128 devices in a mesh: fsdp: 8 (over x, core), seq: 16 (over y, z).
Axes of the slice: x: 4, y: 4, z: 4, core: 2. Of those that a mesh axis runs over, the one named last changes fastest.
Arguments:
- patches: bfloat16 [8192, 4096], P(('fsdp', 'seq')), may hold values from -6 to 6
- image_number: int32 [8192], P('fsdp'), may hold values from 0 to 527, as said below
- patch_grid: int32 [2, 8192], P(None, 'fsdp'), may hold values from 0 to 15, as said below
- first_gain: float32 [4096], replicated, may hold values from 0.25 to 1.75
- first_bias: float32 [4096], replicated, may hold values from -3 to 3
- attend_weight: bfloat16 [4096, 32, 384], P('fsdp', 'seq')
- output_weight: bfloat16 [4096, 4096], P('seq', 'fsdp'), may hold values from -0.09375 to 0.09375
- layer_scale: float32 [4096], replicated, may hold values from 0.25 to 1
- second_gain: float32 [4096], replicated, may hold values from 0.25 to 1.75
- second_bias: float32 [4096], replicated, may hold values from -3 to 3
- merge_weight: bfloat16 [16384, 4096], P('fsdp', 'seq'), may hold values from -0.046875 to 0.046875
- text_rows: bfloat16 [12288, 4096], P(('fsdp', 'seq')), may hold values from -6 to 6
- prompt_source: int32 [12288], P('fsdp'), may hold values from -1 to 255, as said below
- final_gain: float32 [4096], replicated, may hold values from 0.1 to 1.9
- decoder_weight: bfloat16 [4096, 6144], P('fsdp', 'seq'), may hold values from -0.09375 to 0.09375
Outputs:
- vision_rows: bfloat16 [8192, 4096], P(('fsdp', 'seq'))
- projected: bfloat16 [12288, 6144], P('fsdp', 'seq')
The draws below stay inside these ranges and needn't reach their ends.
Inputs may be any that keep to these rules, and one draw needn't show every extreme that they name: `image_number`: images never cross a request group; each image is a grid of 2x2 windows whose four patches stand consecutively (top left, top right, bottom left, bottom right), windows in row order, the last image of a group possibly cut short. `patch_grid`: grid coordinates of a patch within its image. `prompt_source`: within a request group every merged image token takes exactly one prompt row, in increasing order.
All inputs are finite; a program needn't handle non-finite values.
Results may differ from the reference program's by a relative error of at most 0.013.
The reference program's roundings to bfloat16 on the way count: a program that leaves them out, or rounds other values in their place, can miss the bound.
Values may be sent and summed in bfloat16 or wider, within the bound.
No kernel may reach another device: no remote copies, remote signals or barrier semaphores. Data moves between devices by JAX's collectives and lax.ppermute only.
A program may use at most 128 MiB of HBM per device.

```python
import math
import jax
import jax.numpy as jnp
from jax import lax

D = 4096
HEADS = 32
HD = 128
DEC = 4096
QKVD = 6144
PATCHES = 8192
MERGED = 2048
PROMPT = 12288
GROUP = 1024
GROUP_MERGED = 256
GROUP_PROMPT = 1536
HEAD_BLOCK = 2
N_SEQ = 16


def image_layout(key):
    base = jax.random.fold_in(key, 31)
    key_wide, key_tall, key_gaps = jax.random.split(base, 3)
    groups = PATCHES // GROUP
    counts = GROUP_MERGED // 4 + 2
    widths = jax.random.randint(key_wide, (groups, counts), 2, 9)
    heights = jax.random.randint(key_tall, (groups, counts), 2, 9)
    widths = widths.at[:, 0].set(8)
    heights = heights.at[:, 1].set(8)
    areas = widths * heights
    finish = jnp.cumsum(areas, axis=1)
    begins = finish - areas
    window = jnp.arange(GROUP_MERGED, dtype=jnp.int32)
    images = jnp.sum((finish[:, None, :] <= window[None, :, None]).astype(jnp.int32), axis=2)
    local_index = window[None, :] - jnp.take_along_axis(begins, images, axis=1)
    image_width = jnp.take_along_axis(widths, images, axis=1)
    window_row = local_index // image_width
    window_col = local_index % image_width
    return (images, window_row, window_col, key_gaps)


def draw_image_number(key, part):
    images, window_row, window_col, key_gaps = image_layout(key)
    groups = images.shape[0]
    counts = GROUP_MERGED // 4 + 2
    group_ids = jnp.arange(groups, dtype=jnp.int32)[:, None]
    last_image = images[:, -1:]
    lift = jnp.where(group_ids == groups - 1, counts - 1 - last_image, 0)
    numbers = images + lift + group_ids * counts
    return jnp.repeat(numbers, 4, axis=1).reshape(PATCHES).astype(jnp.int32)


def draw_patch_grid(key, part):
    images, window_row, window_col, key_gaps = image_layout(key)
    corner = jnp.arange(4, dtype=jnp.int32)
    grid_rows = 2 * window_row[..., None] + corner // 2
    grid_cols = 2 * window_col[..., None] + corner % 2
    return jnp.stack([grid_rows.reshape(PATCHES), grid_cols.reshape(PATCHES)]).astype(jnp.int32)


def draw_prompt_source(key, part):
    images, window_row, window_col, key_gaps = image_layout(key)
    groups = images.shape[0]
    counts = GROUP_MERGED // 4 + 2
    text_total = GROUP_PROMPT - GROUP_MERGED
    tickets = jax.random.randint(key_gaps, (groups, counts), 1, 16)
    gaps = tickets * text_total // jnp.sum(tickets, axis=1, keepdims=True)
    gap_sums = jnp.cumsum(gaps, axis=1)
    window = jnp.arange(GROUP_MERGED, dtype=jnp.int32)
    target = window[None, :] + jnp.take_along_axis(gap_sums, images, axis=1)
    row_index = jnp.arange(groups, dtype=jnp.int32)[:, None] * GROUP_PROMPT + target
    filled = jnp.broadcast_to(window[None, :], (groups, GROUP_MERGED))
    source = jnp.full((PROMPT,), -1, jnp.int32).at[row_index.reshape(-1)].set(filled.reshape(-1))
    return source


def draw_attend_weight(key, part):
    base = jax.random.fold_in(key, 47)
    key_main = jax.random.fold_in(base, 0)
    values = jax.random.normal(key_main, (D, HEADS, 3 * HD), jnp.float32) * D ** (-0.5)
    return values.astype(jnp.bfloat16)


def block_levels(key, shape, cuts, least, high):
    def one(dim, shards_of):
        draws = jax.random.uniform(jax.random.fold_in(jax.random.fold_in(key, 6), dim), (shards_of,), jnp.float32, least / len(cuts), high / len(cuts))
        return jnp.repeat(jnp.exp(draws), shape[dim] // shards_of).reshape((-1,) + (1,) * (len(shape) - dim - 1))

    level = one(*cuts[0])
    for cut in cuts[1:]:
        level = level * one(*cut)
    return level


def scatter_about(own_key, extent, scale, most, shards=(), kind=jnp.bfloat16):
    values = scale * jax.random.normal(own_key, extent, jnp.float32)
    if shards:
        values = values * block_levels(own_key, extent, shards, -0.22, 0.18)
    return jnp.clip(values, -most, most).astype(kind)


def setup_inputs(seed: int = 0) -> dict:
    key_list = jax.random.split(jax.random.key(seed), 16)
    patches = scatter_about(key_list[0], (PATCHES, D), 1.0, 6.0, ((0, 128),))
    image_number = draw_image_number(jax.random.fold_in(key_list[15], 71), 0)
    patch_grid = draw_patch_grid(jax.random.fold_in(key_list[15], 71), 0)
    first_gain = jnp.clip(1.0 + 0.15 * jax.random.normal(key_list[3], (D,), jnp.float32), 0.25, 1.75)
    first_bias = scatter_about(key_list[4], (D,), 0.5, 3.0, (), jnp.float32)
    attend_weight = draw_attend_weight(jax.random.fold_in(key_list[15], 71), 0)
    output_weight = scatter_about(key_list[6], (D, D), D ** -0.5, 0.09375, ((0, 16), (1, 8)))
    layer_scale = jnp.clip(jnp.exp(jax.random.uniform(key_list[7], (D,), jnp.float32, math.log(0.25), math.log(1.0))), 0.25, 1.0)
    second_gain = jnp.clip(1.0 + 0.15 * jax.random.normal(key_list[8], (D,), jnp.float32), 0.25, 1.75)
    second_bias = scatter_about(key_list[9], (D,), 0.5, 3.0, (), jnp.float32)
    merge_weight = scatter_about(key_list[10], (4 * D, DEC), (4 * D) ** -0.5, 0.046875, ((0, 8), (1, 16)))
    text_rows = scatter_about(key_list[11], (PROMPT, DEC), 1.0, 6.0, ((0, 128),))
    prompt_source = draw_prompt_source(jax.random.fold_in(key_list[15], 71), 0)
    final_gain = jnp.clip(1.0 + 0.18 * jax.random.normal(key_list[13], (DEC,), jnp.float32), 0.1, 1.9)
    decoder_weight = scatter_about(key_list[14], (DEC, QKVD), DEC ** -0.5, 0.09375, ((0, 8), (1, 16)))
    return {"patches": patches, "image_number": image_number, "patch_grid": patch_grid, "first_gain": first_gain, "first_bias": first_bias, "attend_weight": attend_weight, "output_weight": output_weight, "layer_scale": layer_scale, "second_gain": second_gain, "second_bias": second_bias, "merge_weight": merge_weight, "text_rows": text_rows, "prompt_source": prompt_source, "final_gain": final_gain, "decoder_weight": decoder_weight}


def layer_norm(values, factor, shifts):
    center = values - lax.optimization_barrier(jnp.mean(values, axis=-1, keepdims=True))
    spread = lax.optimization_barrier(jnp.mean(center * center, axis=-1, keepdims=True))
    return center * lax.rsqrt(spread + 1e-06) * factor + shifts

def rotate(values, grid_rows, grid_cols):
    quarter = values.shape[-1] // 4
    frequency = 100.0 ** (-jnp.arange(quarter, dtype=jnp.float32) / quarter)
    pieces = []
    for offset, position in ((0, grid_rows), (2 * quarter, grid_cols)):
        angles = position.astype(jnp.float32)[:, None, None] * frequency
        cosine = jnp.cos(angles)
        sine_part = jnp.sin(angles)
        leading = values[..., offset:offset + quarter]
        trailing = values[..., offset + quarter:offset + 2 * quarter]
        pieces.append(leading * cosine - trailing * sine_part)
        pieces.append(leading * sine_part + trailing * cosine)
    return jnp.concatenate(pieces, axis=-1)

def reference(patches, image_number, patch_grid, first_gain, first_bias, attend_weight, output_weight, layer_scale, second_gain, second_bias, merge_weight, text_rows, prompt_source, final_gain, decoder_weight):
    groups = PATCHES // GROUP

    def attend_group(bundle):
        patch_block, numbers, grid = bundle
        inputs = patch_block.astype(jnp.float32)
        normed = layer_norm(inputs, first_gain, first_bias).astype(jnp.bfloat16)
        packed = jnp.dot(normed, attend_weight.reshape(D, HEADS * 3 * HD), preferred_element_type=jnp.float32)
        packed = packed.astype(jnp.bfloat16).reshape(GROUP, HEADS, 3 * HD)
        queries = rotate(packed[..., :HD].astype(jnp.float32), grid[0], grid[1]).astype(jnp.bfloat16)
        keys_turned = rotate(packed[..., HD:2 * HD].astype(jnp.float32), grid[0], grid[1]).astype(jnp.bfloat16)
        values = packed[..., 2 * HD:]
        scores = jnp.einsum('qhd,khd->hqk', queries.astype(jnp.float32), keys_turned.astype(jnp.float32)) / HD ** 0.5
        same_image = numbers[:, None] == numbers[None, :]
        scores = jnp.where(same_image[None], scores, -1e+30)
        peaks = lax.optimization_barrier(jnp.max(scores, axis=-1, keepdims=True))
        expos = jnp.exp(scores - peaks)
        weights = (expos / lax.optimization_barrier(jnp.sum(expos, axis=-1, keepdims=True))).astype(jnp.bfloat16)
        mixed = jnp.einsum('hqk,khd->qhd', weights.astype(jnp.float32), values.astype(jnp.float32))
        mixed = mixed.astype(jnp.bfloat16).reshape(GROUP, HEADS * HD)
        blocks = mixed.reshape(GROUP, N_SEQ, HEAD_BLOCK * HD).transpose(1, 0, 2)
        weight_blocks = output_weight.reshape(N_SEQ, HEAD_BLOCK * HD, D)

        def accumulate(totals, paired):
            block_in, block_weight = paired
            partial_value = jnp.dot(block_in, block_weight, preferred_element_type=jnp.float32).astype(jnp.bfloat16)
            partial_value = lax.optimization_barrier(partial_value)
            return (totals + partial_value.astype(jnp.float32), None)
        summed, unused = lax.scan(accumulate, jnp.zeros((GROUP, D), jnp.float32), (blocks, weight_blocks))
        return (inputs + layer_scale * summed).astype(jnp.bfloat16)
    grids = patch_grid.reshape(2, groups, GROUP).transpose(1, 0, 2)
    vision = lax.map(attend_group, (patches.reshape(groups, GROUP, D), image_number.reshape(groups, GROUP), grids))
    vision_rows = vision.reshape(PATCHES, D)
    merged = layer_norm(vision_rows.astype(jnp.float32), second_gain, second_bias).astype(jnp.bfloat16)
    merged = merged.reshape(MERGED, 4 * D)
    image_tokens = jnp.dot(merged, merge_weight, preferred_element_type=jnp.float32).astype(jnp.bfloat16)
    group_of_row = jnp.arange(PROMPT, dtype=jnp.int32) // GROUP_PROMPT
    lookup = (group_of_row * GROUP_MERGED + jnp.maximum(prompt_source, 0)).astype(jnp.int32)
    prompt = jnp.where(prompt_source[:, None] >= 0, image_tokens[lookup], text_rows)
    realvals = prompt.astype(jnp.float32)
    meansq = lax.optimization_barrier(jnp.mean(realvals * realvals, axis=-1, keepdims=True))
    decoder_in = (realvals * lax.rsqrt(meansq + 1e-05) * final_gain).astype(jnp.bfloat16)
    projected = jnp.dot(decoder_in, decoder_weight, preferred_element_type=jnp.float32).astype(jnp.bfloat16)
    return (vision_rows, projected)
```

```python
import jax
import jax.numpy as jnp
from jax import lax
from jax.sharding import PartitionSpec as P


def layer_norm(values, factor, shifts):
    center = values - jnp.mean(values, axis=-1, keepdims=True)
    spread = jnp.mean(center * center, axis=-1, keepdims=True)
    return center * lax.rsqrt(spread + 1e-06) * factor + shifts


def rms_norm(rows, gain):
    realvals = rows.astype(jnp.float32)
    meansq = jnp.mean(realvals * realvals, axis=-1, keepdims=True)
    return (realvals * lax.rsqrt(meansq + 1e-05) * gain).astype(jnp.bfloat16)


def rotate(values, grid_rows, grid_cols):
    quarter = values.shape[-1] // 4
    frequency = 100.0 ** (-jnp.arange(quarter, dtype=jnp.float32) / quarter)
    pieces = []
    for offset, position in ((0, grid_rows), (2 * quarter, grid_cols)):
        angles = position.astype(jnp.float32)[:, None, None] * frequency
        cosine = jnp.cos(angles)
        sine_part = jnp.sin(angles)
        leading = values[..., offset : offset + quarter]
        trailing = values[..., offset + quarter : offset + 2 * quarter]
        pieces.append(leading * cosine - trailing * sine_part)
        pieces.append(leading * sine_part + trailing * cosine)
    return jnp.concatenate(pieces, axis=-1)


def ring_gather(shard, axis, n):
    me = lax.axis_index(axis)
    forward = [(j, (j + 1) % n) for j in range(n)]
    backward = [(j, (j - 1) % n) for j in range(n)]
    return sub_ring_gather(shard, axis, n, me, forward, backward)


def sub_ring_gather(shard, axis, n, me, forward, backward):
    half = shard.shape[0] // 2
    ahead, behind = shard[:half], shard[half:]
    got_ahead = [ahead]
    got_behind = [behind]
    for _ in range(1, n):
        ahead = lax.ppermute(ahead, axis, forward)
        behind = lax.ppermute(behind, axis, backward)
        got_ahead.append(ahead)
        got_behind.append(behind)
    from_ahead = jnp.stack([got_ahead[(-m) % n] for m in range(n)])
    from_behind = jnp.stack(got_behind)
    from_ahead = jnp.roll(from_ahead, me, axis=0)
    from_behind = jnp.roll(from_behind, me, axis=0)
    return jnp.concatenate([from_ahead, from_behind], axis=1)


def torus_gather(rows, axis, inner):
    total = lax.axis_size(axis)
    outer = total // inner
    me = lax.axis_index(axis)
    me_in, me_out = me % inner, me // inner
    in_fwd = [(j, (j // inner) * inner + (j % inner + 1) % inner) for j in range(total)]
    in_bwd = [(j, (j // inner) * inner + (j % inner - 1) % inner) for j in range(total)]
    out_fwd = [(j, ((j // inner + 1) % outer) * inner + j % inner) for j in range(total)]
    out_bwd = [(j, ((j // inner - 1) % outer) * inner + j % inner) for j in range(total)]
    half = rows.shape[0] // 2
    first, second = rows[:half], rows[half:]
    first = sub_ring_gather(first, axis, inner, me_in, in_fwd, in_bwd)
    first = sub_ring_gather(first, axis, outer, me_out, out_fwd, out_bwd)
    second = sub_ring_gather(second, axis, outer, me_out, out_fwd, out_bwd)
    second = sub_ring_gather(second, axis, inner, me_in, in_fwd, in_bwd)
    second = jnp.swapaxes(second, 0, 1)
    both = jnp.concatenate([first, second], axis=2)
    return both.reshape((total * rows.shape[0],) + rows.shape[1:])


def body(
    patches,
    image_number,
    patch_grid,
    first_gain,
    first_bias,
    attend_weight,
    output_weight,
    layer_scale,
    second_gain,
    second_bias,
    merge_weight,
    text_rows,
    prompt_source,
    final_gain,
    decoder_weight,
):
    fsdp_n = 8
    seq_n = 16
    patch_count = patches.shape[0]
    model_width = patches.shape[1]

    attend_full = ring_gather(attend_weight, "fsdp", fsdp_n)
    attend_full = attend_full.reshape((-1,) + attend_weight.shape[1:])
    output_full = ring_gather(output_weight.T, "fsdp", fsdp_n)
    output_full = output_full.reshape(-1, output_weight.shape[0]).T
    merge_full = ring_gather(merge_weight, "fsdp", fsdp_n)
    merge_full = merge_full.reshape(-1, merge_weight.shape[1])
    decoder_full = ring_gather(decoder_weight, "fsdp", fsdp_n)
    decoder_full = decoder_full.reshape(-1, decoder_weight.shape[1])

    text_normed = rms_norm(text_rows, final_gain)
    text_all = torus_gather(text_normed, "seq", 4)
    text_projected = jnp.dot(text_all, decoder_full, preferred_element_type=jnp.float32)
    text_projected = text_projected.astype(jnp.bfloat16)

    inputs = patches.astype(jnp.float32)
    own_normed = layer_norm(inputs, first_gain, first_bias).astype(jnp.bfloat16)
    normed = lax.all_gather(own_normed, "seq", axis=0, tiled=True)
    group_size = normed.shape[0]
    head_block = attend_weight.shape[1]
    packed_width = attend_weight.shape[2]
    head_size = packed_width // 3
    flat_pieces = attend_full.reshape(attend_full.shape[0], head_block * packed_width)
    packed = jnp.dot(normed, flat_pieces, preferred_element_type=jnp.float32)
    packed = packed.astype(jnp.bfloat16).reshape(group_size, head_block, packed_width)
    queries = rotate(
        packed[..., :head_size].astype(jnp.float32), patch_grid[0], patch_grid[1]
    ).astype(jnp.bfloat16)
    keys_turned = rotate(
        packed[..., head_size : 2 * head_size].astype(jnp.float32), patch_grid[0], patch_grid[1]
    ).astype(jnp.bfloat16)
    values = packed[..., 2 * head_size :]
    scores = (
        jnp.einsum("qhd,khd->hqk", queries, keys_turned, preferred_element_type=jnp.float32)
        / float(head_size) ** 0.5
    )
    same_image = image_number[:, None] == image_number[None, :]
    scores = jnp.where(same_image[None], scores, -1e30)
    peaks = jnp.max(scores, axis=-1, keepdims=True)
    expos = jnp.exp(scores - peaks)
    weights = (expos / jnp.sum(expos, axis=-1, keepdims=True)).astype(jnp.bfloat16)
    mixed = jnp.einsum("hqk,khd->qhd", weights, values, preferred_element_type=jnp.float32)
    mixed = mixed.astype(jnp.bfloat16).reshape(group_size, head_block * head_size)
    partial_value = jnp.dot(mixed, output_full, preferred_element_type=jnp.float32)
    summed = lax.psum_scatter(
        partial_value.astype(jnp.bfloat16), "seq", scatter_dimension=0, tiled=True
    ).astype(jnp.float32)
    vision_rows = (inputs + layer_scale * summed).astype(jnp.bfloat16)
    own_merged = layer_norm(vision_rows.astype(jnp.float32), second_gain, second_bias).astype(
        jnp.bfloat16
    )
    own_merged = own_merged.reshape(patch_count // 4, 4 * model_width)
    merged = lax.all_gather(own_merged, "seq", axis=0, tiled=True)
    image_cols = jnp.dot(merged, merge_full, preferred_element_type=jnp.float32)
    image_cols = image_cols.astype(jnp.bfloat16)
    token_count = image_cols.shape[0]
    image_blocks = lax.all_gather(image_cols, "seq", axis=0, tiled=False)
    image_all = image_blocks.transpose(1, 0, 2).reshape(token_count, seq_n * image_cols.shape[1])

    image_normed = rms_norm(image_all, final_gain)
    image_projected = jnp.dot(image_normed, decoder_full, preferred_element_type=jnp.float32)
    image_projected = image_projected.astype(jnp.bfloat16)
    safe_source = jnp.maximum(prompt_source, 0)
    projected = jnp.where(
        prompt_source[:, None] >= 0, image_projected[safe_source], text_projected
    )
    return (vision_rows, projected)


def solution(mesh):
    return jax.shard_map(
        body,
        mesh=mesh,
        in_specs=(
            P(("fsdp", "seq"), None),
            P("fsdp"),
            P(None, "fsdp"),
            P(),
            P(),
            P("fsdp", "seq", None),
            P("seq", "fsdp"),
            P(),
            P(),
            P(),
            P("fsdp", "seq"),
            P(("fsdp", "seq"), None),
            P("fsdp"),
            P(),
            P("fsdp", "seq"),
        ),
        out_specs=(P(("fsdp", "seq"), None), P("fsdp", "seq")),
        check_vma=False,
    )
```

```python
import jax
import jax.numpy as jnp
from jax import lax
from jax.sharding import PartitionSpec as P


def layer_norm(values, factor, shifts):
    center = values - jnp.mean(values, axis=-1, keepdims=True)
    spread = jnp.mean(center * center, axis=-1, keepdims=True)
    return center * lax.rsqrt(spread + 1e-06) * factor + shifts


def rms_norm(rows, gain):
    realvals = rows.astype(jnp.float32)
    meansq = jnp.mean(realvals * realvals, axis=-1, keepdims=True)
    return (realvals * lax.rsqrt(meansq + 1e-05) * gain).astype(jnp.bfloat16)


def rotate(values, grid_rows, grid_cols):
    quarter = values.shape[-1] // 4
    frequency = 100.0 ** (-jnp.arange(quarter, dtype=jnp.float32) / quarter)
    pieces = []
    for offset, position in ((0, grid_rows), (2 * quarter, grid_cols)):
        angles = position.astype(jnp.float32)[:, None, None] * frequency
        cosine = jnp.cos(angles)
        sine_part = jnp.sin(angles)
        leading = values[..., offset : offset + quarter]
        trailing = values[..., offset + quarter : offset + 2 * quarter]
        pieces.append(leading * cosine - trailing * sine_part)
        pieces.append(leading * sine_part + trailing * cosine)
    return jnp.concatenate(pieces, axis=-1)


def ring_gather(shard, axis, n):
    me = lax.axis_index(axis)
    forward = [(j, (j + 1) % n) for j in range(n)]
    backward = [(j, (j - 1) % n) for j in range(n)]
    return sub_ring_gather(shard, axis, n, me, forward, backward)


def sub_ring_gather(shard, axis, n, me, forward, backward):
    half = shard.shape[0] // 2
    ahead, behind = shard[:half], shard[half:]
    got_ahead = [ahead]
    got_behind = [behind]
    for _ in range(1, n):
        ahead = lax.ppermute(ahead, axis, forward)
        behind = lax.ppermute(behind, axis, backward)
        got_ahead.append(ahead)
        got_behind.append(behind)
    from_ahead = jnp.stack([got_ahead[(-m) % n] for m in range(n)])
    from_behind = jnp.stack(got_behind)
    from_ahead = jnp.roll(from_ahead, me, axis=0)
    from_behind = jnp.roll(from_behind, me, axis=0)
    return jnp.concatenate([from_ahead, from_behind], axis=1)


def torus_gather(rows, axis, inner):
    total = lax.axis_size(axis)
    outer = total // inner
    me = lax.axis_index(axis)
    me_in, me_out = me % inner, me // inner
    in_fwd = [(j, (j // inner) * inner + (j % inner + 1) % inner) for j in range(total)]
    in_bwd = [(j, (j // inner) * inner + (j % inner - 1) % inner) for j in range(total)]
    out_fwd = [(j, ((j // inner + 1) % outer) * inner + j % inner) for j in range(total)]
    out_bwd = [(j, ((j // inner - 1) % outer) * inner + j % inner) for j in range(total)]
    half = rows.shape[0] // 2
    first, second = rows[:half], rows[half:]
    first = sub_ring_gather(first, axis, inner, me_in, in_fwd, in_bwd)
    first = sub_ring_gather(first, axis, outer, me_out, out_fwd, out_bwd)
    second = sub_ring_gather(second, axis, outer, me_out, out_fwd, out_bwd)
    second = sub_ring_gather(second, axis, inner, me_in, in_fwd, in_bwd)
    second = jnp.swapaxes(second, 0, 1)
    both = jnp.concatenate([first, second], axis=2)
    return both.reshape((total * rows.shape[0],) + rows.shape[1:])


def a2a_gather(shard, axis, n):
    copies = jnp.broadcast_to(shard[None], (n,) + shard.shape)
    return lax.all_to_all(copies, axis, 0, 0, tiled=False)


def body(
    patches,
    image_number,
    patch_grid,
    first_gain,
    first_bias,
    attend_weight,
    output_weight,
    layer_scale,
    second_gain,
    second_bias,
    merge_weight,
    text_rows,
    prompt_source,
    final_gain,
    decoder_weight,
):
    fsdp_n = 8
    seq_n = 16
    patch_count = patches.shape[0]
    model_width = patches.shape[1]

    attend_flat = attend_weight.reshape(attend_weight.shape[0], -1)
    attend_full = a2a_gather(attend_flat, "fsdp", fsdp_n).reshape(-1, attend_flat.shape[1])
    output_full = a2a_gather(output_weight.T, "fsdp", fsdp_n)
    output_full = output_full.reshape(-1, output_weight.shape[0]).T
    merge_full = a2a_gather(merge_weight, "fsdp", fsdp_n)
    merge_full = merge_full.reshape(-1, merge_weight.shape[1])
    decoder_full = a2a_gather(decoder_weight, "fsdp", fsdp_n)
    decoder_full = decoder_full.reshape(-1, decoder_weight.shape[1])

    text_normed = rms_norm(text_rows, final_gain)
    text_all = a2a_gather(text_normed, "seq", seq_n).reshape(-1, model_width)
    text_projected = jnp.dot(text_all, decoder_full, preferred_element_type=jnp.float32)
    text_projected = text_projected.astype(jnp.bfloat16)

    inputs = patches.astype(jnp.float32)
    own_normed = layer_norm(inputs, first_gain, first_bias).astype(jnp.bfloat16)
    normed = a2a_gather(own_normed, "seq", seq_n).reshape(-1, model_width)
    group_size = normed.shape[0]
    head_block = attend_weight.shape[1]
    packed_width = attend_weight.shape[2]
    head_size = packed_width // 3
    packed = jnp.dot(normed, attend_full, preferred_element_type=jnp.float32)
    packed = packed.astype(jnp.bfloat16).reshape(group_size, head_block, packed_width)
    queries = rotate(
        packed[..., :head_size].astype(jnp.float32), patch_grid[0], patch_grid[1]
    ).astype(jnp.bfloat16)
    keys_turned = rotate(
        packed[..., head_size : 2 * head_size].astype(jnp.float32), patch_grid[0], patch_grid[1]
    ).astype(jnp.bfloat16)
    values = packed[..., 2 * head_size :]
    scores = (
        jnp.einsum("qhd,khd->hqk", queries, keys_turned, preferred_element_type=jnp.float32)
        / float(head_size) ** 0.5
    )
    same_image = image_number[:, None] == image_number[None, :]
    scores = jnp.where(same_image[None], scores, -1e30)
    peaks = jnp.max(scores, axis=-1, keepdims=True)
    expos = jnp.exp(scores - peaks)
    weights = (expos / jnp.sum(expos, axis=-1, keepdims=True)).astype(jnp.bfloat16)
    mixed = jnp.einsum("hqk,khd->qhd", weights, values, preferred_element_type=jnp.float32)
    mixed = mixed.astype(jnp.bfloat16).reshape(group_size, head_block * head_size)
    partial_value = jnp.dot(mixed, output_full, preferred_element_type=jnp.float32)
    partial_blocks = partial_value.astype(jnp.bfloat16).reshape(seq_n, patch_count, model_width)
    received = lax.all_to_all(partial_blocks, "seq", 0, 0, tiled=False)
    summed = jnp.sum(received.astype(jnp.float32), axis=0)
    vision_rows = (inputs + layer_scale * summed).astype(jnp.bfloat16)
    text_ready = (text_all[0, 0].astype(jnp.float32) + decoder_full[0, 0].astype(jnp.float32)) * 0.0
    own_merged = layer_norm(vision_rows.astype(jnp.float32), second_gain + text_ready, second_bias).astype(
        jnp.bfloat16
    )
    own_merged = own_merged.reshape(patch_count // 4, 4 * model_width)
    merged = a2a_gather(own_merged, "seq", seq_n).reshape(-1, own_merged.shape[1])
    image_cols = jnp.dot(merged, merge_full, preferred_element_type=jnp.float32)
    image_cols = image_cols.astype(jnp.bfloat16)
    token_count = image_cols.shape[0]
    image_blocks = a2a_gather(image_cols, "seq", seq_n)
    image_all = image_blocks.transpose(1, 0, 2).reshape(token_count, seq_n * image_cols.shape[1])

    image_normed = rms_norm(image_all, final_gain)
    image_projected = jnp.dot(image_normed, decoder_full, preferred_element_type=jnp.float32)
    image_projected = image_projected.astype(jnp.bfloat16)
    safe_source = jnp.maximum(prompt_source, 0)
    projected = jnp.where(
        prompt_source[:, None] >= 0, image_projected[safe_source], text_projected
    )
    return (vision_rows, projected)


def solution(mesh):
    return jax.shard_map(
        body,
        mesh=mesh,
        in_specs=(
            P(("fsdp", "seq"), None),
            P("fsdp"),
            P(None, "fsdp"),
            P(),
            P(),
            P("fsdp", "seq", None),
            P("seq", "fsdp"),
            P(),
            P(),
            P(),
            P("fsdp", "seq"),
            P(("fsdp", "seq"), None),
            P("fsdp"),
            P(),
            P("fsdp", "seq"),
        ),
        out_specs=(P(("fsdp", "seq"), None), P("fsdp", "seq")),
        check_vma=False,
    )
```

```python
import jax
import jax.numpy as jnp
from jax import lax
from jax.sharding import PartitionSpec as P


def layer_norm(values, factor, shifts):
    center = values - jnp.mean(values, axis=-1, keepdims=True)
    spread = jnp.mean(center * center, axis=-1, keepdims=True)
    return center * lax.rsqrt(spread + 1e-06) * factor + shifts


def rms_norm(rows, gain):
    realvals = rows.astype(jnp.float32)
    meansq = jnp.mean(realvals * realvals, axis=-1, keepdims=True)
    return (realvals * lax.rsqrt(meansq + 1e-05) * gain).astype(jnp.bfloat16)


def rotate(values, grid_rows, grid_cols):
    quarter = values.shape[-1] // 4
    frequency = 100.0 ** (-jnp.arange(quarter, dtype=jnp.float32) / quarter)
    pieces = []
    for offset, position in ((0, grid_rows), (2 * quarter, grid_cols)):
        angles = position.astype(jnp.float32)[:, None, None] * frequency
        cosine = jnp.cos(angles)
        sine_part = jnp.sin(angles)
        leading = values[..., offset : offset + quarter]
        trailing = values[..., offset + quarter : offset + 2 * quarter]
        pieces.append(leading * cosine - trailing * sine_part)
        pieces.append(leading * sine_part + trailing * cosine)
    return jnp.concatenate(pieces, axis=-1)


def ring_gather(shard, axis, n):
    me = lax.axis_index(axis)
    forward = [(j, (j + 1) % n) for j in range(n)]
    backward = [(j, (j - 1) % n) for j in range(n)]
    return sub_ring_gather(shard, axis, n, me, forward, backward)


def sub_ring_gather(shard, axis, n, me, forward, backward):
    half = shard.shape[0] // 2
    ahead, behind = shard[:half], shard[half:]
    got_ahead = [ahead]
    got_behind = [behind]
    for _ in range(1, n):
        ahead = lax.ppermute(ahead, axis, forward)
        behind = lax.ppermute(behind, axis, backward)
        got_ahead.append(ahead)
        got_behind.append(behind)
    from_ahead = jnp.stack([got_ahead[(-m) % n] for m in range(n)])
    from_behind = jnp.stack(got_behind)
    from_ahead = jnp.roll(from_ahead, me, axis=0)
    from_behind = jnp.roll(from_behind, me, axis=0)
    return jnp.concatenate([from_ahead, from_behind], axis=1)


def torus_gather(rows, axis, inner):
    total = lax.axis_size(axis)
    outer = total // inner
    me = lax.axis_index(axis)
    me_in, me_out = me % inner, me // inner
    in_fwd = [(j, (j // inner) * inner + (j % inner + 1) % inner) for j in range(total)]
    in_bwd = [(j, (j // inner) * inner + (j % inner - 1) % inner) for j in range(total)]
    out_fwd = [(j, ((j // inner + 1) % outer) * inner + j % inner) for j in range(total)]
    out_bwd = [(j, ((j // inner - 1) % outer) * inner + j % inner) for j in range(total)]
    half = rows.shape[0] // 2
    first, second = rows[:half], rows[half:]
    first = sub_ring_gather(first, axis, inner, me_in, in_fwd, in_bwd)
    first = sub_ring_gather(first, axis, outer, me_out, out_fwd, out_bwd)
    second = sub_ring_gather(second, axis, outer, me_out, out_fwd, out_bwd)
    second = sub_ring_gather(second, axis, inner, me_in, in_fwd, in_bwd)
    second = jnp.swapaxes(second, 0, 1)
    both = jnp.concatenate([first, second], axis=2)
    return both.reshape((total * rows.shape[0],) + rows.shape[1:])


def body(
    patches,
    image_number,
    patch_grid,
    first_gain,
    first_bias,
    attend_weight,
    output_weight,
    layer_scale,
    second_gain,
    second_bias,
    merge_weight,
    text_rows,
    prompt_source,
    final_gain,
    decoder_weight,
):
    fsdp_n = 8
    seq_n = 16
    patch_count = patches.shape[0]
    model_width = patches.shape[1]

    attend_flat = attend_weight.reshape(attend_weight.shape[0], -1)
    shard_rows = attend_flat.shape[0]
    pieces = [
        attend_flat,
        output_weight.T,
        merge_weight.reshape(shard_rows, -1),
        decoder_weight,
    ]
    bounds = [0]
    for piece in pieces:
        bounds.append(bounds[-1] + piece.shape[1])
    weights_full = ring_gather(jnp.concatenate(pieces, axis=1), "fsdp", fsdp_n)
    attend_full = weights_full[:, :, bounds[0] : bounds[1]].reshape(-1, attend_flat.shape[1])
    output_full = weights_full[:, :, bounds[1] : bounds[2]].reshape(-1, output_weight.shape[0]).T
    merge_full = weights_full[:, :, bounds[2] : bounds[3]].reshape(-1, merge_weight.shape[1])
    decoder_full = weights_full[:, :, bounds[3] : bounds[4]].reshape(-1, decoder_weight.shape[1])

    text_normed = rms_norm(text_rows, final_gain)

    inputs = patches.astype(jnp.float32)
    own_normed = layer_norm(inputs, first_gain, first_bias).astype(jnp.bfloat16)
    both = jnp.concatenate([own_normed, text_normed], axis=0)
    both_all = lax.all_gather(both, "seq", axis=0, tiled=False)
    normed = both_all[:, :patch_count].reshape(-1, model_width)
    text_all = both_all[:, patch_count:].reshape(-1, model_width)
    text_projected = jnp.dot(text_all, decoder_full, preferred_element_type=jnp.float32)
    text_projected = text_projected.astype(jnp.bfloat16)
    group_size = normed.shape[0]
    head_block = attend_weight.shape[1]
    packed_width = attend_weight.shape[2]
    head_size = packed_width // 3
    packed = jnp.dot(normed, attend_full, preferred_element_type=jnp.float32)
    packed = packed.astype(jnp.bfloat16).reshape(group_size, head_block, packed_width)
    queries = rotate(
        packed[..., :head_size].astype(jnp.float32), patch_grid[0], patch_grid[1]
    ).astype(jnp.bfloat16)
    keys_turned = rotate(
        packed[..., head_size : 2 * head_size].astype(jnp.float32), patch_grid[0], patch_grid[1]
    ).astype(jnp.bfloat16)
    values = packed[..., 2 * head_size :]
    scores = (
        jnp.einsum("qhd,khd->hqk", queries, keys_turned, preferred_element_type=jnp.float32)
        / float(head_size) ** 0.5
    )
    same_image = image_number[:, None] == image_number[None, :]
    scores = jnp.where(same_image[None], scores, -1e30)
    peaks = jnp.max(scores, axis=-1, keepdims=True)
    expos = jnp.exp(scores - peaks)
    weights = (expos / jnp.sum(expos, axis=-1, keepdims=True)).astype(jnp.bfloat16)
    mixed = jnp.einsum("hqk,khd->qhd", weights, values, preferred_element_type=jnp.float32)
    mixed = mixed.astype(jnp.bfloat16).reshape(group_size, head_block * head_size)
    partial_value = jnp.dot(mixed, output_full, preferred_element_type=jnp.float32)
    summed = lax.psum_scatter(
        partial_value.astype(jnp.bfloat16), "seq", scatter_dimension=0, tiled=True
    ).astype(jnp.float32)
    vision_rows = (inputs + layer_scale * summed).astype(jnp.bfloat16)
    own_merged = layer_norm(vision_rows.astype(jnp.float32), second_gain, second_bias).astype(
        jnp.bfloat16
    )
    own_merged = own_merged.reshape(patch_count // 4, 4 * model_width)
    merged = lax.all_gather(own_merged, "seq", axis=0, tiled=True)
    image_cols = jnp.dot(merged, merge_full, preferred_element_type=jnp.float32)
    image_cols = image_cols.astype(jnp.bfloat16)
    token_count = image_cols.shape[0]
    image_blocks = lax.all_gather(image_cols, "seq", axis=0, tiled=False)
    image_all = image_blocks.transpose(1, 0, 2).reshape(token_count, seq_n * image_cols.shape[1])

    image_normed = rms_norm(image_all, final_gain)
    image_projected = jnp.dot(image_normed, decoder_full, preferred_element_type=jnp.float32)
    image_projected = image_projected.astype(jnp.bfloat16)
    safe_source = jnp.maximum(prompt_source, 0)
    projected = jnp.where(
        prompt_source[:, None] >= 0, image_projected[safe_source], text_projected
    )
    return (vision_rows, projected)


def solution(mesh):
    return jax.shard_map(
        body,
        mesh=mesh,
        in_specs=(
            P(("fsdp", "seq"), None),
            P("fsdp"),
            P(None, "fsdp"),
            P(),
            P(),
            P("fsdp", "seq", None),
            P("seq", "fsdp"),
            P(),
            P(),
            P(),
            P("fsdp", "seq"),
            P(("fsdp", "seq"), None),
            P("fsdp"),
            P(),
            P("fsdp", "seq"),
        ),
        out_specs=(P(("fsdp", "seq"), None), P("fsdp", "seq")),
        check_vma=False,
    )
```

```python
import jax
import jax.numpy as jnp
from jax import lax
from jax.sharding import PartitionSpec as P


def layer_norm(values, factor, shifts):
    center = values - jnp.mean(values, axis=-1, keepdims=True)
    spread = jnp.mean(center * center, axis=-1, keepdims=True)
    return center * lax.rsqrt(spread + 1e-06) * factor + shifts


def rms_norm(rows, gain):
    realvals = rows.astype(jnp.float32)
    meansq = jnp.mean(realvals * realvals, axis=-1, keepdims=True)
    return (realvals * lax.rsqrt(meansq + 1e-05) * gain).astype(jnp.bfloat16)


def rotate(values, grid_rows, grid_cols):
    quarter = values.shape[-1] // 4
    frequency = 100.0 ** (-jnp.arange(quarter, dtype=jnp.float32) / quarter)
    pieces = []
    for offset, position in ((0, grid_rows), (2 * quarter, grid_cols)):
        angles = position.astype(jnp.float32)[:, None, None] * frequency
        cosine = jnp.cos(angles)
        sine_part = jnp.sin(angles)
        leading = values[..., offset : offset + quarter]
        trailing = values[..., offset + quarter : offset + 2 * quarter]
        pieces.append(leading * cosine - trailing * sine_part)
        pieces.append(leading * sine_part + trailing * cosine)
    return jnp.concatenate(pieces, axis=-1)


def ring_gather(shard, axis, n):
    me = lax.axis_index(axis)
    forward = [(j, (j + 1) % n) for j in range(n)]
    backward = [(j, (j - 1) % n) for j in range(n)]
    return sub_ring_gather(shard, axis, n, me, forward, backward)


def sub_ring_gather(shard, axis, n, me, forward, backward):
    half = shard.shape[0] // 2
    ahead, behind = shard[:half], shard[half:]
    got_ahead = [ahead]
    got_behind = [behind]
    for _ in range(1, n):
        ahead = lax.ppermute(ahead, axis, forward)
        behind = lax.ppermute(behind, axis, backward)
        got_ahead.append(ahead)
        got_behind.append(behind)
    from_ahead = jnp.stack([got_ahead[(-m) % n] for m in range(n)])
    from_behind = jnp.stack(got_behind)
    from_ahead = jnp.roll(from_ahead, me, axis=0)
    from_behind = jnp.roll(from_behind, me, axis=0)
    return jnp.concatenate([from_ahead, from_behind], axis=1)


def torus_gather(rows, axis, inner):
    total = lax.axis_size(axis)
    outer = total // inner
    me = lax.axis_index(axis)
    me_in, me_out = me % inner, me // inner
    in_fwd = [(j, (j // inner) * inner + (j % inner + 1) % inner) for j in range(total)]
    in_bwd = [(j, (j // inner) * inner + (j % inner - 1) % inner) for j in range(total)]
    out_fwd = [(j, ((j // inner + 1) % outer) * inner + j % inner) for j in range(total)]
    out_bwd = [(j, ((j // inner - 1) % outer) * inner + j % inner) for j in range(total)]
    half = rows.shape[0] // 2
    first, second = rows[:half], rows[half:]
    first = sub_ring_gather(first, axis, inner, me_in, in_fwd, in_bwd)
    first = sub_ring_gather(first, axis, outer, me_out, out_fwd, out_bwd)
    second = sub_ring_gather(second, axis, outer, me_out, out_fwd, out_bwd)
    second = sub_ring_gather(second, axis, inner, me_in, in_fwd, in_bwd)
    second = jnp.swapaxes(second, 0, 1)
    both = jnp.concatenate([first, second], axis=2)
    return both.reshape((total * rows.shape[0],) + rows.shape[1:])


def body(
    patches,
    image_number,
    patch_grid,
    first_gain,
    first_bias,
    attend_weight,
    output_weight,
    layer_scale,
    second_gain,
    second_bias,
    merge_weight,
    text_rows,
    prompt_source,
    final_gain,
    decoder_weight,
):
    fsdp_n = 8
    seq_n = 16
    patch_count = patches.shape[0]
    model_width = patches.shape[1]

    attend_flat = attend_weight.reshape(attend_weight.shape[0], -1)
    shard_rows = attend_flat.shape[0]
    pieces = [
        attend_flat,
        output_weight.T,
        merge_weight.reshape(shard_rows, -1),
        decoder_weight,
    ]
    bounds = [0]
    for piece in pieces:
        bounds.append(bounds[-1] + piece.shape[1])
    weights_full = ring_gather(jnp.concatenate(pieces, axis=1), "fsdp", fsdp_n)
    attend_full = weights_full[:, :, bounds[0] : bounds[1]].reshape(-1, attend_flat.shape[1])
    output_full = weights_full[:, :, bounds[1] : bounds[2]].reshape(-1, output_weight.shape[0]).T
    merge_full = weights_full[:, :, bounds[2] : bounds[3]].reshape(-1, merge_weight.shape[1])
    decoder_full = weights_full[:, :, bounds[3] : bounds[4]].reshape(-1, decoder_weight.shape[1])

    text_normed = rms_norm(text_rows, final_gain)

    inputs = patches.astype(jnp.float32)
    own_normed = layer_norm(inputs, first_gain, first_bias).astype(jnp.bfloat16)
    both = jnp.concatenate([own_normed, text_normed], axis=0)
    both_all = lax.all_gather(both, "seq", axis=0, tiled=False)
    normed_blocks = both_all[:, :patch_count]
    text_all = both_all[:, patch_count:].reshape(-1, model_width)
    text_projected = jnp.dot(text_all, decoder_full, preferred_element_type=jnp.float32)
    text_projected = text_projected.astype(jnp.bfloat16)
    group_size = seq_n * patch_count
    head_block = attend_weight.shape[1]
    packed_width = attend_weight.shape[2]
    head_size = packed_width // 3
    packed = jnp.einsum(
        "spd,dk->spk", normed_blocks, attend_full, preferred_element_type=jnp.float32
    )
    packed = packed.astype(jnp.bfloat16).reshape(group_size, head_block, packed_width)
    queries = rotate(
        packed[..., :head_size].astype(jnp.float32), patch_grid[0], patch_grid[1]
    ).astype(jnp.bfloat16)
    keys_turned = rotate(
        packed[..., head_size : 2 * head_size].astype(jnp.float32), patch_grid[0], patch_grid[1]
    ).astype(jnp.bfloat16)
    values = packed[..., 2 * head_size :]
    scores = (
        jnp.einsum("qhd,khd->hqk", queries, keys_turned, preferred_element_type=jnp.float32)
        / float(head_size) ** 0.5
    )
    same_image = image_number[:, None] == image_number[None, :]
    scores = jnp.where(same_image[None], scores, -1e30)
    peaks = jnp.max(scores, axis=-1, keepdims=True)
    expos = jnp.exp(scores - peaks)
    weights = (expos / jnp.sum(expos, axis=-1, keepdims=True)).astype(jnp.bfloat16)
    mixed = jnp.einsum("hqk,khd->qhd", weights, values, preferred_element_type=jnp.float32)
    mixed = mixed.astype(jnp.bfloat16).reshape(group_size, head_block * head_size)
    partial_value = jnp.dot(mixed, output_full, preferred_element_type=jnp.float32)
    summed = lax.psum_scatter(
        partial_value.astype(jnp.bfloat16), "seq", scatter_dimension=0, tiled=True
    ).astype(jnp.float32)
    vision_rows = (inputs + layer_scale * summed).astype(jnp.bfloat16)
    own_merged = layer_norm(vision_rows.astype(jnp.float32), second_gain, second_bias).astype(
        jnp.bfloat16
    )
    own_merged = own_merged.reshape(patch_count // 4, 4 * model_width)
    merged = lax.all_gather(own_merged, "seq", axis=0, tiled=True)
    image_cols = jnp.dot(merged, merge_full, preferred_element_type=jnp.float32)
    image_cols = image_cols.astype(jnp.bfloat16)
    token_count = image_cols.shape[0]
    block_width = image_cols.shape[1]
    image_blocks = lax.all_gather(image_cols, "seq", axis=0, tiled=False)
    image_real = image_blocks.astype(jnp.float32)
    image_meansq = jnp.mean(image_real * image_real, axis=(0, 2), keepdims=True)
    image_normed = (
        image_real
        * lax.rsqrt(image_meansq + 1e-05)
        * final_gain.reshape(seq_n, 1, block_width)
    ).astype(jnp.bfloat16)
    image_projected = jnp.einsum(
        "stc,scn->tn",
        image_normed,
        decoder_full.reshape(seq_n, block_width, -1),
        preferred_element_type=jnp.float32,
    ).astype(jnp.bfloat16)
    is_image = prompt_source[:, None] >= 0
    pick = (prompt_source[:, None] == jnp.arange(token_count)[None, :]).astype(jnp.bfloat16)
    image_rows = jnp.dot(pick, image_projected, preferred_element_type=jnp.float32)
    projected = jnp.where(is_image, image_rows.astype(jnp.bfloat16), text_projected)
    return (vision_rows, projected)


def solution(mesh):
    return jax.shard_map(
        body,
        mesh=mesh,
        in_specs=(
            P(("fsdp", "seq"), None),
            P("fsdp"),
            P(None, "fsdp"),
            P(),
            P(),
            P("fsdp", "seq", None),
            P("seq", "fsdp"),
            P(),
            P(),
            P(),
            P("fsdp", "seq"),
            P(("fsdp", "seq"), None),
            P("fsdp"),
            P(),
            P("fsdp", "seq"),
        ),
        out_specs=(P(("fsdp", "seq"), None), P("fsdp", "seq")),
        check_vma=False,
    )
```

```python
import jax
import jax.numpy as jnp
from jax import lax
from jax.sharding import PartitionSpec as P


def layer_norm(values, factor, shifts):
    center = values - jnp.mean(values, axis=-1, keepdims=True)
    spread = jnp.mean(center * center, axis=-1, keepdims=True)
    return center * lax.rsqrt(spread + 1e-06) * factor + shifts


def rms_norm(rows, gain):
    realvals = rows.astype(jnp.float32)
    meansq = jnp.mean(realvals * realvals, axis=-1, keepdims=True)
    return (realvals * lax.rsqrt(meansq + 1e-05) * gain).astype(jnp.bfloat16)


def rotate(values, grid_rows, grid_cols):
    quarter = values.shape[-1] // 4
    frequency = 100.0 ** (-jnp.arange(quarter, dtype=jnp.float32) / quarter)
    pieces = []
    for offset, position in ((0, grid_rows), (2 * quarter, grid_cols)):
        angles = position.astype(jnp.float32)[:, None, None] * frequency
        cosine = jnp.cos(angles)
        sine_part = jnp.sin(angles)
        leading = values[..., offset : offset + quarter]
        trailing = values[..., offset + quarter : offset + 2 * quarter]
        pieces.append(leading * cosine - trailing * sine_part)
        pieces.append(leading * sine_part + trailing * cosine)
    return jnp.concatenate(pieces, axis=-1)


def ring_gather(shard, axis, n):
    me = lax.axis_index(axis)
    forward = [(j, (j + 1) % n) for j in range(n)]
    backward = [(j, (j - 1) % n) for j in range(n)]
    return sub_ring_gather(shard, axis, n, me, forward, backward)


def sub_ring_gather(shard, axis, n, me, forward, backward):
    half = shard.shape[0] // 2
    ahead, behind = shard[:half], shard[half:]
    got_ahead = [ahead]
    got_behind = [behind]
    for _ in range(1, n):
        ahead = lax.ppermute(ahead, axis, forward)
        behind = lax.ppermute(behind, axis, backward)
        got_ahead.append(ahead)
        got_behind.append(behind)
    from_ahead = jnp.stack([got_ahead[(-m) % n] for m in range(n)])
    from_behind = jnp.stack(got_behind)
    from_ahead = jnp.roll(from_ahead, me, axis=0)
    from_behind = jnp.roll(from_behind, me, axis=0)
    return jnp.concatenate([from_ahead, from_behind], axis=1)


def torus_gather(rows, axis, inner):
    total = lax.axis_size(axis)
    outer = total // inner
    me = lax.axis_index(axis)
    me_in, me_out = me % inner, me // inner
    in_fwd = [(j, (j // inner) * inner + (j % inner + 1) % inner) for j in range(total)]
    in_bwd = [(j, (j // inner) * inner + (j % inner - 1) % inner) for j in range(total)]
    out_fwd = [(j, ((j // inner + 1) % outer) * inner + j % inner) for j in range(total)]
    out_bwd = [(j, ((j // inner - 1) % outer) * inner + j % inner) for j in range(total)]
    half = rows.shape[0] // 2
    first, second = rows[:half], rows[half:]
    first = sub_ring_gather(first, axis, inner, me_in, in_fwd, in_bwd)
    first = sub_ring_gather(first, axis, outer, me_out, out_fwd, out_bwd)
    second = sub_ring_gather(second, axis, outer, me_out, out_fwd, out_bwd)
    second = sub_ring_gather(second, axis, inner, me_in, in_fwd, in_bwd)
    second = jnp.swapaxes(second, 0, 1)
    both = jnp.concatenate([first, second], axis=2)
    return both.reshape((total * rows.shape[0],) + rows.shape[1:])


def body(
    patches,
    image_number,
    patch_grid,
    first_gain,
    first_bias,
    attend_weight,
    output_weight,
    layer_scale,
    second_gain,
    second_bias,
    merge_weight,
    text_rows,
    prompt_source,
    final_gain,
    decoder_weight,
):
    fsdp_n = 8
    seq_n = 16
    patch_count = patches.shape[0]
    model_width = patches.shape[1]

    attend_flat = attend_weight.reshape(attend_weight.shape[0], -1)
    attend_cols = attend_flat.shape[1]
    shard_rows = attend_flat.shape[0]
    early = jnp.concatenate([attend_flat, output_weight.T], axis=1)
    early_full = ring_gather(early, "fsdp", fsdp_n)
    attend_full = early_full[:, :, :attend_cols].reshape(-1, attend_cols)
    output_full = early_full[:, :, attend_cols:].reshape(-1, output_weight.shape[0]).T
    text_normed = rms_norm(text_rows, final_gain)

    inputs = patches.astype(jnp.float32)
    own_normed = layer_norm(inputs, first_gain, first_bias).astype(jnp.bfloat16)
    normed = lax.all_gather(own_normed, "seq", axis=0, tiled=True)
    after_normed = own_normed[0, 0] * 0
    text_all = lax.all_gather(text_normed + after_normed, "seq", axis=0, tiled=True)
    group_size = seq_n * patch_count
    head_block = attend_weight.shape[1]
    packed_width = attend_weight.shape[2]
    head_size = packed_width // 3
    packed = jnp.dot(normed, attend_full, preferred_element_type=jnp.float32)
    merge_cols = merge_weight.size // shard_rows
    late = jnp.concatenate([merge_weight.reshape(shard_rows, merge_cols), decoder_weight], axis=1)
    late = late + (packed[0, 0] * 0).astype(late.dtype)
    late_full = ring_gather(late, "fsdp", fsdp_n)
    merge_full = late_full[:, :, :merge_cols].reshape(-1, merge_weight.shape[1])
    decoder_full = late_full[:, :, merge_cols:].reshape(-1, decoder_weight.shape[1])

    after_text = (text_all[0, 0] * 0).astype(jnp.float32) + ((late_full[0, 0, 0] + late_full[0, -1, 0]) * 0).astype(jnp.float32)
    text_projected = jnp.dot(text_all, decoder_full, preferred_element_type=jnp.float32)
    text_projected = text_projected.astype(jnp.bfloat16)
    packed = packed.astype(jnp.bfloat16).reshape(group_size, head_block, packed_width)
    queries = rotate(
        packed[..., :head_size].astype(jnp.float32), patch_grid[0], patch_grid[1]
    ).astype(jnp.bfloat16)
    keys_turned = rotate(
        packed[..., head_size : 2 * head_size].astype(jnp.float32), patch_grid[0], patch_grid[1]
    ).astype(jnp.bfloat16)
    values = packed[..., 2 * head_size :]
    scores = (
        jnp.einsum("qhd,khd->hqk", queries, keys_turned, preferred_element_type=jnp.float32)
        / float(head_size) ** 0.5
    )
    same_image = image_number[:, None] == image_number[None, :]
    scores = jnp.where(same_image[None], scores, -1e30)
    peaks = jnp.max(scores, axis=-1, keepdims=True)
    expos = jnp.exp(scores - peaks)
    weights = (expos / jnp.sum(expos, axis=-1, keepdims=True)).astype(jnp.bfloat16)
    mixed = jnp.einsum("hqk,khd->qhd", weights, values, preferred_element_type=jnp.float32)
    mixed = mixed.astype(jnp.bfloat16).reshape(group_size, head_block * head_size)
    partial_value = jnp.dot(mixed, output_full, preferred_element_type=jnp.float32) + after_text
    summed = lax.psum_scatter(
        partial_value.astype(jnp.bfloat16), "seq", scatter_dimension=0, tiled=True
    ).astype(jnp.float32)
    vision_rows = (inputs + layer_scale * summed).astype(jnp.bfloat16)
    own_merged = layer_norm(vision_rows.astype(jnp.float32), second_gain, second_bias).astype(
        jnp.bfloat16
    )
    own_merged = own_merged.reshape(patch_count // 4, 4 * model_width)
    merged = lax.all_gather(own_merged, "seq", axis=0, tiled=True)
    image_cols = jnp.dot(merged, merge_full, preferred_element_type=jnp.float32)
    image_cols = image_cols.astype(jnp.bfloat16)
    token_count = image_cols.shape[0]
    block_width = image_cols.shape[1]
    image_blocks = lax.all_gather(image_cols, "seq", axis=0, tiled=False)
    image_real = image_blocks.astype(jnp.float32)
    image_meansq = jnp.mean(image_real * image_real, axis=(0, 2), keepdims=True)
    image_normed = (
        image_real
        * lax.rsqrt(image_meansq + 1e-05)
        * final_gain.reshape(seq_n, 1, block_width)
    ).astype(jnp.bfloat16)
    image_projected = jnp.einsum(
        "stc,scn->tn",
        image_normed,
        decoder_full.reshape(seq_n, block_width, -1),
        preferred_element_type=jnp.float32,
    ).astype(jnp.bfloat16)
    is_image = prompt_source[:, None] >= 0
    pick = (prompt_source[:, None] == jnp.arange(token_count)[None, :]).astype(jnp.bfloat16)
    image_rows = jnp.dot(pick, image_projected, preferred_element_type=jnp.float32)
    projected = jnp.where(is_image, image_rows.astype(jnp.bfloat16), text_projected)
    return (vision_rows, projected)


def solution(mesh):
    return jax.shard_map(
        body,
        mesh=mesh,
        in_specs=(
            P(("fsdp", "seq"), None),
            P("fsdp"),
            P(None, "fsdp"),
            P(),
            P(),
            P("fsdp", "seq", None),
            P("seq", "fsdp"),
            P(),
            P(),
            P(),
            P("fsdp", "seq"),
            P(("fsdp", "seq"), None),
            P("fsdp"),
            P(),
            P("fsdp", "seq"),
        ),
        out_specs=(P(("fsdp", "seq"), None), P("fsdp", "seq")),
        check_vma=False,
    )
```

```python
import jax
import jax.numpy as jnp
from jax import lax
from jax.sharding import PartitionSpec as P


def layer_norm(values, factor, shifts):
    center = values - jnp.mean(values, axis=-1, keepdims=True)
    spread = jnp.mean(center * center, axis=-1, keepdims=True)
    return center * lax.rsqrt(spread + 1e-06) * factor + shifts


def rms_norm(rows, gain):
    realvals = rows.astype(jnp.float32)
    meansq = jnp.mean(realvals * realvals, axis=-1, keepdims=True)
    return (realvals * lax.rsqrt(meansq + 1e-05) * gain).astype(jnp.bfloat16)


def rotate(values, grid_rows, grid_cols):
    quarter = values.shape[-1] // 4
    frequency = 100.0 ** (-jnp.arange(quarter, dtype=jnp.float32) / quarter)
    pieces = []
    for offset, position in ((0, grid_rows), (2 * quarter, grid_cols)):
        angles = position.astype(jnp.float32)[:, None, None] * frequency
        cosine = jnp.cos(angles)
        sine_part = jnp.sin(angles)
        leading = values[..., offset : offset + quarter]
        trailing = values[..., offset + quarter : offset + 2 * quarter]
        pieces.append(leading * cosine - trailing * sine_part)
        pieces.append(leading * sine_part + trailing * cosine)
    return jnp.concatenate(pieces, axis=-1)


def ring_gather(shard, axis, n):
    me = lax.axis_index(axis)
    forward = [(j, (j + 1) % n) for j in range(n)]
    backward = [(j, (j - 1) % n) for j in range(n)]
    return sub_ring_gather(shard, axis, n, me, forward, backward)


def sub_ring_gather(shard, axis, n, me, forward, backward):
    half = shard.shape[0] // 2
    ahead, behind = shard[:half], shard[half:]
    got_ahead = [ahead]
    got_behind = [behind]
    for _ in range(1, n):
        ahead = lax.ppermute(ahead, axis, forward)
        behind = lax.ppermute(behind, axis, backward)
        got_ahead.append(ahead)
        got_behind.append(behind)
    from_ahead = jnp.stack([got_ahead[(-m) % n] for m in range(n)])
    from_behind = jnp.stack(got_behind)
    from_ahead = jnp.roll(from_ahead, me, axis=0)
    from_behind = jnp.roll(from_behind, me, axis=0)
    return jnp.concatenate([from_ahead, from_behind], axis=1)


def torus_gather(rows, axis, inner):
    total = lax.axis_size(axis)
    outer = total // inner
    me = lax.axis_index(axis)
    me_in, me_out = me % inner, me // inner
    in_fwd = [(j, (j // inner) * inner + (j % inner + 1) % inner) for j in range(total)]
    in_bwd = [(j, (j // inner) * inner + (j % inner - 1) % inner) for j in range(total)]
    out_fwd = [(j, ((j // inner + 1) % outer) * inner + j % inner) for j in range(total)]
    out_bwd = [(j, ((j // inner - 1) % outer) * inner + j % inner) for j in range(total)]
    half = rows.shape[0] // 2
    first, second = rows[:half], rows[half:]
    first = sub_ring_gather(first, axis, inner, me_in, in_fwd, in_bwd)
    first = sub_ring_gather(first, axis, outer, me_out, out_fwd, out_bwd)
    second = sub_ring_gather(second, axis, outer, me_out, out_fwd, out_bwd)
    second = sub_ring_gather(second, axis, inner, me_in, in_fwd, in_bwd)
    second = jnp.swapaxes(second, 0, 1)
    both = jnp.concatenate([first, second], axis=2)
    return both.reshape((total * rows.shape[0],) + rows.shape[1:])


def body(
    patches,
    image_number,
    patch_grid,
    first_gain,
    first_bias,
    attend_weight,
    output_weight,
    layer_scale,
    second_gain,
    second_bias,
    merge_weight,
    text_rows,
    prompt_source,
    final_gain,
    decoder_weight,
):
    fsdp_n = 8
    seq_n = 16
    patch_count = patches.shape[0]
    model_width = patches.shape[1]

    attend_flat = attend_weight.reshape(attend_weight.shape[0], -1)
    attend_cols = attend_flat.shape[1]
    shard_rows = attend_flat.shape[0]
    early = jnp.concatenate([attend_flat, output_weight.T], axis=1)
    early_full = ring_gather(early, "fsdp", fsdp_n)
    attend_full = early_full[:, :, :attend_cols].reshape(-1, attend_cols)
    output_full = early_full[:, :, attend_cols:].reshape(-1, output_weight.shape[0]).T
    text_normed = rms_norm(text_rows, final_gain)

    inputs = patches.astype(jnp.float32)
    own_normed = layer_norm(inputs, first_gain, first_bias).astype(jnp.bfloat16)
    normed = lax.all_gather(own_normed, "seq", axis=0, tiled=True)
    after_normed = own_normed[0, 0] * 0
    text_all = lax.all_gather(text_normed + after_normed, "seq", axis=0, tiled=True)
    group_size = seq_n * patch_count
    head_block = attend_weight.shape[1]
    packed_width = attend_weight.shape[2]
    head_size = packed_width // 3
    packed = jnp.dot(normed, attend_full, preferred_element_type=jnp.float32)
    packed = packed.astype(jnp.bfloat16).reshape(group_size, head_block, packed_width)
    queries = rotate(
        packed[..., :head_size].astype(jnp.float32), patch_grid[0], patch_grid[1]
    ).astype(jnp.bfloat16)
    keys_turned = rotate(
        packed[..., head_size : 2 * head_size].astype(jnp.float32), patch_grid[0], patch_grid[1]
    ).astype(jnp.bfloat16)
    values = packed[..., 2 * head_size :]
    scores = (
        jnp.einsum("qhd,khd->hqk", queries, keys_turned, preferred_element_type=jnp.float32)
        / float(head_size) ** 0.5
    )
    same_image = image_number[:, None] == image_number[None, :]
    scores = jnp.where(same_image[None], scores, -1e30)
    peaks = jnp.max(scores, axis=-1, keepdims=True)
    expos = jnp.exp(scores - peaks)
    weights = (expos / jnp.sum(expos, axis=-1, keepdims=True)).astype(jnp.bfloat16)
    mixed = jnp.einsum("hqk,khd->qhd", weights, values, preferred_element_type=jnp.float32)
    mixed = mixed.astype(jnp.bfloat16).reshape(group_size, head_block * head_size)
    after_text = (text_all[0, 0] * 0).astype(jnp.float32)
    partial_value = jnp.dot(mixed, output_full, preferred_element_type=jnp.float32) + after_text
    merge_cols = merge_weight.size // shard_rows
    late = jnp.concatenate([merge_weight.reshape(shard_rows, merge_cols), decoder_weight], axis=1)
    late = late + (partial_value[0, 0] * 0).astype(late.dtype)
    late_full = ring_gather(late, "fsdp", fsdp_n)
    merge_full = late_full[:, :, :merge_cols].reshape(-1, merge_weight.shape[1])
    decoder_full = late_full[:, :, merge_cols:].reshape(-1, decoder_weight.shape[1])

    text_projected = jnp.dot(text_all, decoder_full, preferred_element_type=jnp.float32)
    text_projected = text_projected.astype(jnp.bfloat16)
    summed = lax.psum_scatter(
        partial_value.astype(jnp.bfloat16), "seq", scatter_dimension=0, tiled=True
    ).astype(jnp.float32)
    vision_rows = (inputs + layer_scale * summed).astype(jnp.bfloat16)
    after_late = ((late_full[0, 0, 0] + late_full[0, -1, 0]) * 0).astype(jnp.float32)
    own_merged = layer_norm(vision_rows.astype(jnp.float32), second_gain + after_late, second_bias).astype(
        jnp.bfloat16
    )
    own_merged = own_merged.reshape(patch_count // 4, 4 * model_width)
    merged = lax.all_gather(own_merged, "seq", axis=0, tiled=True)
    image_cols = jnp.dot(merged, merge_full, preferred_element_type=jnp.float32)
    image_cols = image_cols.astype(jnp.bfloat16)
    token_count = image_cols.shape[0]
    block_width = image_cols.shape[1]
    image_blocks = lax.all_gather(image_cols, "seq", axis=0, tiled=False)
    image_real = image_blocks.astype(jnp.float32)
    image_meansq = jnp.mean(image_real * image_real, axis=(0, 2), keepdims=True)
    image_normed = (
        image_real
        * lax.rsqrt(image_meansq + 1e-05)
        * final_gain.reshape(seq_n, 1, block_width)
    ).astype(jnp.bfloat16)
    image_projected = jnp.einsum(
        "stc,scn->tn",
        image_normed,
        decoder_full.reshape(seq_n, block_width, -1),
        preferred_element_type=jnp.float32,
    ).astype(jnp.bfloat16)
    is_image = prompt_source[:, None] >= 0
    pick = (prompt_source[:, None] == jnp.arange(token_count)[None, :]).astype(jnp.bfloat16)
    image_rows = jnp.dot(pick, image_projected, preferred_element_type=jnp.float32)
    projected = jnp.where(is_image, image_rows.astype(jnp.bfloat16), text_projected)
    return (vision_rows, projected)


def solution(mesh):
    return jax.shard_map(
        body,
        mesh=mesh,
        in_specs=(
            P(("fsdp", "seq"), None),
            P("fsdp"),
            P(None, "fsdp"),
            P(),
            P(),
            P("fsdp", "seq", None),
            P("seq", "fsdp"),
            P(),
            P(),
            P(),
            P("fsdp", "seq"),
            P(("fsdp", "seq"), None),
            P("fsdp"),
            P(),
            P("fsdp", "seq"),
        ),
        out_specs=(P(("fsdp", "seq"), None), P("fsdp", "seq")),
        check_vma=False,
    )
```

```python
import jax
import jax.numpy as jnp
from jax import lax
from jax.sharding import PartitionSpec as P


def layer_norm(values, factor, shifts):
    center = values - jnp.mean(values, axis=-1, keepdims=True)
    spread = jnp.mean(center * center, axis=-1, keepdims=True)
    return center * lax.rsqrt(spread + 1e-06) * factor + shifts


def rms_norm(rows, gain):
    realvals = rows.astype(jnp.float32)
    meansq = jnp.mean(realvals * realvals, axis=-1, keepdims=True)
    return (realvals * lax.rsqrt(meansq + 1e-05) * gain).astype(jnp.bfloat16)


def rotate(values, grid_rows, grid_cols):
    quarter = values.shape[-1] // 4
    frequency = 100.0 ** (-jnp.arange(quarter, dtype=jnp.float32) / quarter)
    pieces = []
    for offset, position in ((0, grid_rows), (2 * quarter, grid_cols)):
        angles = position.astype(jnp.float32)[:, None, None] * frequency
        cosine = jnp.cos(angles)
        sine_part = jnp.sin(angles)
        leading = values[..., offset : offset + quarter]
        trailing = values[..., offset + quarter : offset + 2 * quarter]
        pieces.append(leading * cosine - trailing * sine_part)
        pieces.append(leading * sine_part + trailing * cosine)
    return jnp.concatenate(pieces, axis=-1)


def ring_gather(shard, axis, n):
    me = lax.axis_index(axis)
    forward = [(j, (j + 1) % n) for j in range(n)]
    backward = [(j, (j - 1) % n) for j in range(n)]
    return sub_ring_gather(shard, axis, n, me, forward, backward)


def sub_ring_gather(shard, axis, n, me, forward, backward):
    half = shard.shape[0] // 2
    ahead, behind = shard[:half], shard[half:]
    got_ahead = [ahead]
    got_behind = [behind]
    for _ in range(1, n):
        ahead = lax.ppermute(ahead, axis, forward)
        behind = lax.ppermute(behind, axis, backward)
        got_ahead.append(ahead)
        got_behind.append(behind)
    from_ahead = jnp.stack([got_ahead[(-m) % n] for m in range(n)])
    from_behind = jnp.stack(got_behind)
    from_ahead = jnp.roll(from_ahead, me, axis=0)
    from_behind = jnp.roll(from_behind, me, axis=0)
    return jnp.concatenate([from_ahead, from_behind], axis=1)


def torus_gather(rows, axis, inner):
    total = lax.axis_size(axis)
    outer = total // inner
    me = lax.axis_index(axis)
    me_in, me_out = me % inner, me // inner
    in_fwd = [(j, (j // inner) * inner + (j % inner + 1) % inner) for j in range(total)]
    in_bwd = [(j, (j // inner) * inner + (j % inner - 1) % inner) for j in range(total)]
    out_fwd = [(j, ((j // inner + 1) % outer) * inner + j % inner) for j in range(total)]
    out_bwd = [(j, ((j // inner - 1) % outer) * inner + j % inner) for j in range(total)]
    half = rows.shape[0] // 2
    first, second = rows[:half], rows[half:]
    first = sub_ring_gather(first, axis, inner, me_in, in_fwd, in_bwd)
    first = sub_ring_gather(first, axis, outer, me_out, out_fwd, out_bwd)
    second = sub_ring_gather(second, axis, outer, me_out, out_fwd, out_bwd)
    second = sub_ring_gather(second, axis, inner, me_in, in_fwd, in_bwd)
    second = jnp.swapaxes(second, 0, 1)
    both = jnp.concatenate([first, second], axis=2)
    return both.reshape((total * rows.shape[0],) + rows.shape[1:])


def body(
    patches,
    image_number,
    patch_grid,
    first_gain,
    first_bias,
    attend_weight,
    output_weight,
    layer_scale,
    second_gain,
    second_bias,
    merge_weight,
    text_rows,
    prompt_source,
    final_gain,
    decoder_weight,
):
    fsdp_n = 8
    seq_n = 16
    patch_count = patches.shape[0]
    model_width = patches.shape[1]

    attend_flat = attend_weight.reshape(attend_weight.shape[0], -1)
    attend_cols = attend_flat.shape[1]
    shard_rows = attend_flat.shape[0]
    output_end = attend_cols + output_weight.shape[0]
    early = jnp.concatenate([attend_flat, output_weight.T, decoder_weight], axis=1)
    early_full = ring_gather(early, "fsdp", fsdp_n)
    attend_full = early_full[:, :, :attend_cols].reshape(-1, attend_cols)
    output_full = early_full[:, :, attend_cols:output_end].reshape(-1, output_weight.shape[0]).T
    decoder_full = early_full[:, :, output_end:].reshape(-1, decoder_weight.shape[1])
    text_normed = rms_norm(text_rows, final_gain)

    inputs = patches.astype(jnp.float32)
    own_normed = layer_norm(inputs, first_gain, first_bias).astype(jnp.bfloat16)
    normed = lax.all_gather(own_normed, "seq", axis=0, tiled=True)
    after_normed = own_normed[0, 0] * 0
    text_all = lax.all_gather(text_normed + after_normed, "seq", axis=0, tiled=True)
    group_size = seq_n * patch_count
    head_block = attend_weight.shape[1]
    packed_width = attend_weight.shape[2]
    head_size = packed_width // 3
    packed = jnp.dot(normed, attend_full, preferred_element_type=jnp.float32)
    packed = packed.astype(jnp.bfloat16).reshape(group_size, head_block, packed_width)
    queries = rotate(
        packed[..., :head_size].astype(jnp.float32), patch_grid[0], patch_grid[1]
    ).astype(jnp.bfloat16)
    keys_turned = rotate(
        packed[..., head_size : 2 * head_size].astype(jnp.float32), patch_grid[0], patch_grid[1]
    ).astype(jnp.bfloat16)
    values = packed[..., 2 * head_size :]
    scores = (
        jnp.einsum("qhd,khd->hqk", queries, keys_turned, preferred_element_type=jnp.float32)
        / float(head_size) ** 0.5
    )
    same_image = image_number[:, None] == image_number[None, :]
    scores = jnp.where(same_image[None], scores, -1e30)
    peaks = jnp.max(scores, axis=-1, keepdims=True)
    expos = jnp.exp(scores - peaks)
    weights = (expos / jnp.sum(expos, axis=-1, keepdims=True)).astype(jnp.bfloat16)
    mixed = jnp.einsum("hqk,khd->qhd", weights, values, preferred_element_type=jnp.float32)
    mixed = mixed.astype(jnp.bfloat16).reshape(group_size, head_block * head_size)
    after_text = (text_all[0, 0] * 0).astype(jnp.float32)
    partial_value = jnp.dot(mixed, output_full, preferred_element_type=jnp.float32) + after_text
    merge_cols = merge_weight.size // shard_rows
    late = merge_weight.reshape(shard_rows, merge_cols)
    late = late + (partial_value[0, 0] * 0).astype(late.dtype)
    late_full = ring_gather(late, "fsdp", fsdp_n)
    merge_full = late_full.reshape(-1, merge_weight.shape[1])

    text_projected = jnp.dot(text_all, decoder_full, preferred_element_type=jnp.float32)
    text_projected = text_projected.astype(jnp.bfloat16)
    summed = lax.psum_scatter(
        partial_value.astype(jnp.bfloat16), "seq", scatter_dimension=0, tiled=True
    ).astype(jnp.float32)
    vision_rows = (inputs + layer_scale * summed).astype(jnp.bfloat16)
    after_late = ((late_full[0, 0, 0] + late_full[0, -1, 0]) * 0).astype(jnp.float32)
    own_merged = layer_norm(vision_rows.astype(jnp.float32), second_gain + after_late, second_bias).astype(
        jnp.bfloat16
    )
    own_merged = own_merged.reshape(patch_count // 4, 4 * model_width)
    merged = lax.all_gather(own_merged, "seq", axis=0, tiled=True)
    image_cols = jnp.dot(merged, merge_full, preferred_element_type=jnp.float32)
    image_cols = image_cols.astype(jnp.bfloat16)
    token_count = image_cols.shape[0]
    block_width = image_cols.shape[1]
    image_blocks = lax.all_gather(image_cols, "seq", axis=0, tiled=False)
    image_real = image_blocks.astype(jnp.float32)
    image_meansq = jnp.mean(image_real * image_real, axis=(0, 2), keepdims=True)
    image_normed = (
        image_real
        * lax.rsqrt(image_meansq + 1e-05)
        * final_gain.reshape(seq_n, 1, block_width)
    ).astype(jnp.bfloat16)
    image_projected = jnp.einsum(
        "stc,scn->tn",
        image_normed,
        decoder_full.reshape(seq_n, block_width, -1),
        preferred_element_type=jnp.float32,
    ).astype(jnp.bfloat16)
    is_image = prompt_source[:, None] >= 0
    pick = (prompt_source[:, None] == jnp.arange(token_count)[None, :]).astype(jnp.bfloat16)
    image_rows = jnp.dot(pick, image_projected, preferred_element_type=jnp.float32)
    projected = jnp.where(is_image, image_rows.astype(jnp.bfloat16), text_projected)
    return (vision_rows, projected)


def solution(mesh):
    return jax.shard_map(
        body,
        mesh=mesh,
        in_specs=(
            P(("fsdp", "seq"), None),
            P("fsdp"),
            P(None, "fsdp"),
            P(),
            P(),
            P("fsdp", "seq", None),
            P("seq", "fsdp"),
            P(),
            P(),
            P(),
            P("fsdp", "seq"),
            P(("fsdp", "seq"), None),
            P("fsdp"),
            P(),
            P("fsdp", "seq"),
        ),
        out_specs=(P(("fsdp", "seq"), None), P("fsdp", "seq")),
        check_vma=False,
    )
```

```python
import jax
import jax.numpy as jnp
from jax import lax
from jax.sharding import PartitionSpec as P


def layer_norm(values, factor, shifts):
    center = values - jnp.mean(values, axis=-1, keepdims=True)
    spread = jnp.mean(center * center, axis=-1, keepdims=True)
    return center * lax.rsqrt(spread + 1e-06) * factor + shifts


def rms_norm(rows, gain):
    realvals = rows.astype(jnp.float32)
    meansq = jnp.mean(realvals * realvals, axis=-1, keepdims=True)
    return (realvals * lax.rsqrt(meansq + 1e-05) * gain).astype(jnp.bfloat16)


def rotate(values, grid_rows, grid_cols):
    quarter = values.shape[-1] // 4
    frequency = 100.0 ** (-jnp.arange(quarter, dtype=jnp.float32) / quarter)
    pieces = []
    for offset, position in ((0, grid_rows), (2 * quarter, grid_cols)):
        angles = position.astype(jnp.float32)[:, None, None] * frequency
        cosine = jnp.cos(angles)
        sine_part = jnp.sin(angles)
        leading = values[..., offset : offset + quarter]
        trailing = values[..., offset + quarter : offset + 2 * quarter]
        pieces.append(leading * cosine - trailing * sine_part)
        pieces.append(leading * sine_part + trailing * cosine)
    return jnp.concatenate(pieces, axis=-1)


def ring_gather(shard, axis, n, bounds=None):
    me = lax.axis_index(axis)
    forward = [(j, (j + 1) % n) for j in range(n)]
    backward = [(j, (j - 1) % n) for j in range(n)]
    half = shard.shape[0] // 2
    ahead, behind = shard[:half], shard[half:]
    got_ahead = [ahead]
    got_behind = [behind]
    for _ in range(1, n):
        ahead = lax.ppermute(ahead, axis, forward)
        behind = lax.ppermute(behind, axis, backward)
        got_ahead.append(ahead)
        got_behind.append(behind)
    if bounds is None:
        bounds = [0, shard.shape[-1]]
    results = []
    for lo, hi in zip(bounds[:-1], bounds[1:]):
        from_ahead = jnp.stack([got_ahead[(-m) % n][..., lo:hi] for m in range(n)])
        from_behind = jnp.stack([got_behind[m][..., lo:hi] for m in range(n)])
        from_ahead = jnp.roll(from_ahead, me, axis=0)
        from_behind = jnp.roll(from_behind, me, axis=0)
        results.append(jnp.concatenate([from_ahead, from_behind], axis=1))
    return results


def sub_ring_gather(shard, axis, n, me, forward, backward):
    half = shard.shape[0] // 2
    ahead, behind = shard[:half], shard[half:]
    got_ahead = [ahead]
    got_behind = [behind]
    for _ in range(1, n):
        ahead = lax.ppermute(ahead, axis, forward)
        behind = lax.ppermute(behind, axis, backward)
        got_ahead.append(ahead)
        got_behind.append(behind)
    from_ahead = jnp.stack([got_ahead[(-m) % n] for m in range(n)])
    from_behind = jnp.stack(got_behind)
    from_ahead = jnp.roll(from_ahead, me, axis=0)
    from_behind = jnp.roll(from_behind, me, axis=0)
    return jnp.concatenate([from_ahead, from_behind], axis=1)


def torus_gather(rows, axis, inner):
    total = lax.axis_size(axis)
    outer = total // inner
    me = lax.axis_index(axis)
    me_in, me_out = me % inner, me // inner
    in_fwd = [(j, (j // inner) * inner + (j % inner + 1) % inner) for j in range(total)]
    in_bwd = [(j, (j // inner) * inner + (j % inner - 1) % inner) for j in range(total)]
    out_fwd = [(j, ((j // inner + 1) % outer) * inner + j % inner) for j in range(total)]
    out_bwd = [(j, ((j // inner - 1) % outer) * inner + j % inner) for j in range(total)]
    half = rows.shape[0] // 2
    first, second = rows[:half], rows[half:]
    first = sub_ring_gather(first, axis, inner, me_in, in_fwd, in_bwd)
    first = sub_ring_gather(first, axis, outer, me_out, out_fwd, out_bwd)
    second = sub_ring_gather(second, axis, outer, me_out, out_fwd, out_bwd)
    second = sub_ring_gather(second, axis, inner, me_in, in_fwd, in_bwd)
    second = jnp.swapaxes(second, 0, 1)
    both = jnp.concatenate([first, second], axis=2)
    return both.reshape((total * rows.shape[0],) + rows.shape[1:])


def body(
    patches,
    image_number,
    patch_grid,
    first_gain,
    first_bias,
    attend_weight,
    output_weight,
    layer_scale,
    second_gain,
    second_bias,
    merge_weight,
    text_rows,
    prompt_source,
    final_gain,
    decoder_weight,
):
    fsdp_n = 8
    seq_n = 16
    patch_count = patches.shape[0]
    model_width = patches.shape[1]

    attend_flat = attend_weight.reshape(attend_weight.shape[0], -1)
    attend_cols = attend_flat.shape[1]
    shard_rows = attend_flat.shape[0]
    output_end = attend_cols + output_weight.shape[0]
    early = jnp.concatenate([attend_flat, output_weight.T, decoder_weight], axis=1)
    early_full, decoder_full = ring_gather(
        early, "fsdp", fsdp_n, [0, output_end, early.shape[1]]
    )
    attend_full = early_full[:, :, :attend_cols].reshape(-1, attend_cols)
    output_full = early_full[:, :, attend_cols:].reshape(-1, output_weight.shape[0]).T
    text_normed = rms_norm(text_rows, final_gain)

    inputs = patches.astype(jnp.float32)
    own_normed = layer_norm(inputs, first_gain, first_bias).astype(jnp.bfloat16)
    normed = lax.all_gather(own_normed, "seq", axis=0, tiled=True)
    after_normed = own_normed[0, 0] * 0
    text_all = lax.all_gather(text_normed + after_normed, "seq", axis=0, tiled=True)
    group_size = seq_n * patch_count
    head_block = attend_weight.shape[1]
    packed_width = attend_weight.shape[2]
    head_size = packed_width // 3
    packed = jnp.dot(normed, attend_full, preferred_element_type=jnp.float32)
    decoder_full = decoder_full + (packed[0, 0] * 0).astype(decoder_full.dtype)
    decoder_full = decoder_full.reshape(-1, decoder_weight.shape[1])
    packed = packed.astype(jnp.bfloat16).reshape(group_size, head_block, packed_width)
    queries = rotate(
        packed[..., :head_size].astype(jnp.float32), patch_grid[0], patch_grid[1]
    ).astype(jnp.bfloat16)
    keys_turned = rotate(
        packed[..., head_size : 2 * head_size].astype(jnp.float32), patch_grid[0], patch_grid[1]
    ).astype(jnp.bfloat16)
    values = packed[..., 2 * head_size :]
    scores = (
        jnp.einsum("qhd,khd->hqk", queries, keys_turned, preferred_element_type=jnp.float32)
        / float(head_size) ** 0.5
    )
    same_image = image_number[:, None] == image_number[None, :]
    scores = jnp.where(same_image[None], scores, -1e30)
    peaks = jnp.max(scores, axis=-1, keepdims=True)
    expos = jnp.exp(scores - peaks)
    weights = (expos / jnp.sum(expos, axis=-1, keepdims=True)).astype(jnp.bfloat16)
    mixed = jnp.einsum("hqk,khd->qhd", weights, values, preferred_element_type=jnp.float32)
    mixed = mixed.astype(jnp.bfloat16).reshape(group_size, head_block * head_size)
    after_text = (text_all[0, 0] * 0).astype(jnp.float32)
    partial_value = jnp.dot(mixed, output_full, preferred_element_type=jnp.float32) + after_text
    merge_cols = merge_weight.size // shard_rows
    late = merge_weight.reshape(shard_rows, merge_cols)
    partial_sent = partial_value.astype(jnp.bfloat16)
    late = late + partial_sent[0, 0] * 0
    (late_full,) = ring_gather(late, "fsdp", fsdp_n)
    merge_full = late_full.reshape(-1, merge_weight.shape[1])

    text_projected = jnp.dot(text_all, decoder_full, preferred_element_type=jnp.float32)
    text_projected = text_projected.astype(jnp.bfloat16)
    summed = lax.psum_scatter(
        partial_sent, "seq", scatter_dimension=0, tiled=True
    ).astype(jnp.float32)
    vision_rows = (inputs + layer_scale * summed).astype(jnp.bfloat16)
    after_late = ((late_full[0, 0, 0] + late_full[0, -1, 0]) * 0).astype(jnp.float32)
    own_merged = layer_norm(vision_rows.astype(jnp.float32), second_gain + after_late, second_bias).astype(
        jnp.bfloat16
    )
    own_merged = own_merged.reshape(patch_count // 4, 4 * model_width)
    merged = lax.all_gather(own_merged, "seq", axis=0, tiled=True)
    image_cols = jnp.dot(merged, merge_full, preferred_element_type=jnp.float32)
    image_cols = image_cols.astype(jnp.bfloat16)
    token_count = image_cols.shape[0]
    block_width = image_cols.shape[1]
    image_blocks = lax.all_gather(image_cols, "seq", axis=0, tiled=False)
    image_real = image_blocks.astype(jnp.float32)
    image_meansq = jnp.mean(image_real * image_real, axis=(0, 2), keepdims=True)
    image_normed = (
        image_real
        * lax.rsqrt(image_meansq + 1e-05)
        * final_gain.reshape(seq_n, 1, block_width)
    ).astype(jnp.bfloat16)
    image_projected = jnp.einsum(
        "stc,scn->tn",
        image_normed,
        decoder_full.reshape(seq_n, block_width, -1),
        preferred_element_type=jnp.float32,
    ).astype(jnp.bfloat16)
    is_image = prompt_source[:, None] >= 0
    pick = (prompt_source[:, None] == jnp.arange(token_count)[None, :]).astype(jnp.bfloat16)
    image_rows = jnp.dot(pick, image_projected, preferred_element_type=jnp.float32)
    projected = jnp.where(is_image, image_rows.astype(jnp.bfloat16), text_projected)
    return (vision_rows, projected)


def solution(mesh):
    return jax.shard_map(
        body,
        mesh=mesh,
        in_specs=(
            P(("fsdp", "seq"), None),
            P("fsdp"),
            P(None, "fsdp"),
            P(),
            P(),
            P("fsdp", "seq", None),
            P("seq", "fsdp"),
            P(),
            P(),
            P(),
            P("fsdp", "seq"),
            P(("fsdp", "seq"), None),
            P("fsdp"),
            P(),
            P("fsdp", "seq"),
        ),
        out_specs=(P(("fsdp", "seq"), None), P("fsdp", "seq")),
        check_vma=False,
    )
```

```python
import jax
import jax.numpy as jnp
from jax import lax
from jax.sharding import PartitionSpec as P


def layer_norm(values, factor, shifts):
    center = values - jnp.mean(values, axis=-1, keepdims=True)
    spread = jnp.mean(center * center, axis=-1, keepdims=True)
    return center * lax.rsqrt(spread + 1e-06) * factor + shifts


def rms_norm(rows, gain):
    realvals = rows.astype(jnp.float32)
    meansq = jnp.mean(realvals * realvals, axis=-1, keepdims=True)
    return (realvals * lax.rsqrt(meansq + 1e-05) * gain).astype(jnp.bfloat16)


def rotate(values, grid_rows, grid_cols):
    quarter = values.shape[-1] // 4
    frequency = 100.0 ** (-jnp.arange(quarter, dtype=jnp.float32) / quarter)
    pieces = []
    for offset, position in ((0, grid_rows), (2 * quarter, grid_cols)):
        angles = position.astype(jnp.float32)[:, None, None] * frequency
        cosine = jnp.cos(angles)
        sine_part = jnp.sin(angles)
        leading = values[..., offset : offset + quarter]
        trailing = values[..., offset + quarter : offset + 2 * quarter]
        pieces.append(leading * cosine - trailing * sine_part)
        pieces.append(leading * sine_part + trailing * cosine)
    return jnp.concatenate(pieces, axis=-1)


def ring_gather(shard, axis, n, bounds=None):
    me = lax.axis_index(axis)
    forward = [(j, (j + 1) % n) for j in range(n)]
    backward = [(j, (j - 1) % n) for j in range(n)]
    half = shard.shape[0] // 2
    ahead, behind = shard[:half], shard[half:]
    got_ahead = [ahead]
    got_behind = [behind]
    for _ in range(1, n):
        ahead = lax.ppermute(ahead, axis, forward)
        behind = lax.ppermute(behind, axis, backward)
        got_ahead.append(ahead)
        got_behind.append(behind)
    if bounds is None:
        bounds = [0, shard.shape[-1]]
    results = []
    for lo, hi in zip(bounds[:-1], bounds[1:]):
        from_ahead = jnp.stack([got_ahead[(-m) % n][..., lo:hi] for m in range(n)])
        from_behind = jnp.stack([got_behind[m][..., lo:hi] for m in range(n)])
        from_ahead = jnp.roll(from_ahead, me, axis=0)
        from_behind = jnp.roll(from_behind, me, axis=0)
        results.append(jnp.concatenate([from_ahead, from_behind], axis=1))
    return results


def sub_ring_gather(shard, axis, n, me, forward, backward):
    half = shard.shape[0] // 2
    ahead, behind = shard[:half], shard[half:]
    got_ahead = [ahead]
    got_behind = [behind]
    for _ in range(1, n):
        ahead = lax.ppermute(ahead, axis, forward)
        behind = lax.ppermute(behind, axis, backward)
        got_ahead.append(ahead)
        got_behind.append(behind)
    from_ahead = jnp.stack([got_ahead[(-m) % n] for m in range(n)])
    from_behind = jnp.stack(got_behind)
    from_ahead = jnp.roll(from_ahead, me, axis=0)
    from_behind = jnp.roll(from_behind, me, axis=0)
    return jnp.concatenate([from_ahead, from_behind], axis=1)


def torus_gather(rows, axis, inner):
    total = lax.axis_size(axis)
    outer = total // inner
    me = lax.axis_index(axis)
    me_in, me_out = me % inner, me // inner
    in_fwd = [(j, (j // inner) * inner + (j % inner + 1) % inner) for j in range(total)]
    in_bwd = [(j, (j // inner) * inner + (j % inner - 1) % inner) for j in range(total)]
    out_fwd = [(j, ((j // inner + 1) % outer) * inner + j % inner) for j in range(total)]
    out_bwd = [(j, ((j // inner - 1) % outer) * inner + j % inner) for j in range(total)]
    half = rows.shape[0] // 2
    first, second = rows[:half], rows[half:]
    first = sub_ring_gather(first, axis, inner, me_in, in_fwd, in_bwd)
    first = sub_ring_gather(first, axis, outer, me_out, out_fwd, out_bwd)
    second = sub_ring_gather(second, axis, outer, me_out, out_fwd, out_bwd)
    second = sub_ring_gather(second, axis, inner, me_in, in_fwd, in_bwd)
    second = jnp.swapaxes(second, 0, 1)
    both = jnp.concatenate([first, second], axis=2)
    return both.reshape((total * rows.shape[0],) + rows.shape[1:])


def body(
    patches,
    image_number,
    patch_grid,
    first_gain,
    first_bias,
    attend_weight,
    output_weight,
    layer_scale,
    second_gain,
    second_bias,
    merge_weight,
    text_rows,
    prompt_source,
    final_gain,
    decoder_weight,
):
    fsdp_n = 8
    seq_n = 16
    patch_count = patches.shape[0]
    model_width = patches.shape[1]

    attend_flat = attend_weight.reshape(attend_weight.shape[0], -1)
    attend_cols = attend_flat.shape[1]
    shard_rows = attend_flat.shape[0]
    output_end = attend_cols + output_weight.shape[0]
    early = jnp.concatenate([attend_flat, output_weight.T, decoder_weight], axis=1)
    early_full, decoder_full = ring_gather(
        early, "fsdp", fsdp_n, [0, output_end, early.shape[1]]
    )
    attend_full = early_full[:, :, :attend_cols].reshape(-1, attend_cols)
    output_full = early_full[:, :, attend_cols:].reshape(-1, output_weight.shape[0]).T
    text_normed = rms_norm(text_rows, final_gain)

    inputs = patches.astype(jnp.float32)
    own_normed = layer_norm(inputs, first_gain, first_bias).astype(jnp.bfloat16)
    normed = lax.all_gather(own_normed, "seq", axis=0, tiled=True)
    after_normed = own_normed[0, 0] * 0
    text_all = lax.all_gather(text_normed + after_normed, "seq", axis=0, tiled=True)
    group_size = seq_n * patch_count
    head_block = attend_weight.shape[1]
    packed_width = attend_weight.shape[2]
    head_size = packed_width // 3
    packed = jnp.dot(normed, attend_full, preferred_element_type=jnp.float32)
    decoder_full = decoder_full + (packed[0, 0] * 0).astype(decoder_full.dtype)
    decoder_full = decoder_full.reshape(-1, decoder_weight.shape[1])
    packed = packed.astype(jnp.bfloat16).reshape(group_size, head_block, packed_width)
    queries = rotate(
        packed[..., :head_size].astype(jnp.float32), patch_grid[0], patch_grid[1]
    ).astype(jnp.bfloat16)
    keys_turned = rotate(
        packed[..., head_size : 2 * head_size].astype(jnp.float32), patch_grid[0], patch_grid[1]
    ).astype(jnp.bfloat16)
    values = packed[..., 2 * head_size :]
    scores = (
        jnp.einsum("qhd,khd->hqk", queries, keys_turned, preferred_element_type=jnp.float32)
        / float(head_size) ** 0.5
    )
    same_image = image_number[:, None] == image_number[None, :]
    scores = jnp.where(same_image[None], scores, -1e30)
    peaks = jnp.max(scores, axis=-1, keepdims=True)
    expos = jnp.exp(scores - peaks)
    weights = (expos / jnp.sum(expos, axis=-1, keepdims=True)).astype(jnp.bfloat16)
    mixed = jnp.einsum("hqk,khd->qhd", weights, values, preferred_element_type=jnp.float32)
    mixed = mixed.astype(jnp.bfloat16).reshape(group_size, head_block * head_size)
    partial_value = jnp.dot(mixed, output_full, preferred_element_type=jnp.float32)
    merge_cols = merge_weight.size // shard_rows
    late = merge_weight.reshape(shard_rows, merge_cols)
    partial_sent = partial_value.astype(jnp.bfloat16)
    corner = partial_sent[:1, :1] + text_all[:1, :1] * 0
    partial_sent = lax.dynamic_update_slice(partial_sent, corner, (0, 0))
    late = late + partial_sent[0, 0] * 0
    (late_full,) = ring_gather(late, "fsdp", fsdp_n)
    merge_full = late_full.reshape(-1, merge_weight.shape[1])

    text_projected = jnp.dot(text_all, decoder_full, preferred_element_type=jnp.float32)
    text_projected = text_projected.astype(jnp.bfloat16)
    summed = lax.psum_scatter(
        partial_sent, "seq", scatter_dimension=0, tiled=True
    ).astype(jnp.float32)
    vision_rows = (inputs + layer_scale * summed).astype(jnp.bfloat16)
    after_late = ((late_full[0, 0, 0] + late_full[0, -1, 0]) * 0).astype(jnp.float32)
    own_merged = layer_norm(vision_rows.astype(jnp.float32), second_gain + after_late, second_bias).astype(
        jnp.bfloat16
    )
    own_merged = own_merged.reshape(patch_count // 4, 4 * model_width)
    merged = lax.all_gather(own_merged, "seq", axis=0, tiled=True)
    image_cols = jnp.dot(merged, merge_full, preferred_element_type=jnp.float32)
    image_cols = image_cols.astype(jnp.bfloat16)
    token_count = image_cols.shape[0]
    block_width = image_cols.shape[1]
    image_blocks = lax.all_gather(image_cols, "seq", axis=0, tiled=False)
    image_real = image_blocks.astype(jnp.float32)
    image_meansq = jnp.mean(image_real * image_real, axis=(0, 2), keepdims=True)
    image_normed = (
        image_real
        * lax.rsqrt(image_meansq + 1e-05)
        * final_gain.reshape(seq_n, 1, block_width)
    ).astype(jnp.bfloat16)
    image_projected = jnp.einsum(
        "stc,scn->tn",
        image_normed,
        decoder_full.reshape(seq_n, block_width, -1),
        preferred_element_type=jnp.float32,
    ).astype(jnp.bfloat16)
    is_image = prompt_source[:, None] >= 0
    pick = (prompt_source[:, None] == jnp.arange(token_count)[None, :]).astype(jnp.bfloat16)
    image_rows = jnp.dot(pick, image_projected, preferred_element_type=jnp.float32)
    projected = jnp.where(is_image, image_rows.astype(jnp.bfloat16), text_projected)
    return (vision_rows, projected)


def solution(mesh):
    return jax.shard_map(
        body,
        mesh=mesh,
        in_specs=(
            P(("fsdp", "seq"), None),
            P("fsdp"),
            P(None, "fsdp"),
            P(),
            P(),
            P("fsdp", "seq", None),
            P("seq", "fsdp"),
            P(),
            P(),
            P(),
            P("fsdp", "seq"),
            P(("fsdp", "seq"), None),
            P("fsdp"),
            P(),
            P("fsdp", "seq"),
        ),
        out_specs=(P(("fsdp", "seq"), None), P("fsdp", "seq")),
        check_vma=False,
    )
```

```python
import jax
import jax.numpy as jnp
from jax import lax
from jax.sharding import PartitionSpec as P


def layer_norm(values, factor, shifts):
    center = values - jnp.mean(values, axis=-1, keepdims=True)
    spread = jnp.mean(center * center, axis=-1, keepdims=True)
    return center * lax.rsqrt(spread + 1e-06) * factor + shifts


def rms_norm(rows, gain):
    realvals = rows.astype(jnp.float32)
    meansq = jnp.mean(realvals * realvals, axis=-1, keepdims=True)
    return (realvals * lax.rsqrt(meansq + 1e-05) * gain).astype(jnp.bfloat16)


def rotate(values, grid_rows, grid_cols):
    quarter = values.shape[-1] // 4
    frequency = 100.0 ** (-jnp.arange(quarter, dtype=jnp.float32) / quarter)
    pieces = []
    for offset, position in ((0, grid_rows), (2 * quarter, grid_cols)):
        angles = position.astype(jnp.float32)[:, None, None] * frequency
        cosine = jnp.cos(angles)
        sine_part = jnp.sin(angles)
        leading = values[..., offset : offset + quarter]
        trailing = values[..., offset + quarter : offset + 2 * quarter]
        pieces.append(leading * cosine - trailing * sine_part)
        pieces.append(leading * sine_part + trailing * cosine)
    return jnp.concatenate(pieces, axis=-1)


def ring_gather(shard, axis, n, bounds=None):
    me = lax.axis_index(axis)
    forward = [(j, (j + 1) % n) for j in range(n)]
    backward = [(j, (j - 1) % n) for j in range(n)]
    half = shard.shape[0] // 2
    ahead, behind = shard[:half], shard[half:]
    got_ahead = [ahead]
    got_behind = [behind]
    for _ in range(1, n):
        ahead = lax.ppermute(ahead, axis, forward)
        behind = lax.ppermute(behind, axis, backward)
        got_ahead.append(ahead)
        got_behind.append(behind)
    if bounds is None:
        bounds = [0, shard.shape[-1]]
    results = []
    for lo, hi in zip(bounds[:-1], bounds[1:]):
        from_ahead = jnp.stack([got_ahead[(-m) % n][..., lo:hi] for m in range(n)])
        from_behind = jnp.stack([got_behind[m][..., lo:hi] for m in range(n)])
        from_ahead = jnp.roll(from_ahead, me, axis=0)
        from_behind = jnp.roll(from_behind, me, axis=0)
        results.append(jnp.concatenate([from_ahead, from_behind], axis=1))
    return results


def sub_ring_gather(shard, axis, n, me, forward, backward):
    half = shard.shape[0] // 2
    ahead, behind = shard[:half], shard[half:]
    got_ahead = [ahead]
    got_behind = [behind]
    for _ in range(1, n):
        ahead = lax.ppermute(ahead, axis, forward)
        behind = lax.ppermute(behind, axis, backward)
        got_ahead.append(ahead)
        got_behind.append(behind)
    from_ahead = jnp.stack([got_ahead[(-m) % n] for m in range(n)])
    from_behind = jnp.stack(got_behind)
    from_ahead = jnp.roll(from_ahead, me, axis=0)
    from_behind = jnp.roll(from_behind, me, axis=0)
    return jnp.concatenate([from_ahead, from_behind], axis=1)


def torus_gather(rows, axis, inner):
    total = lax.axis_size(axis)
    outer = total // inner
    me = lax.axis_index(axis)
    me_in, me_out = me % inner, me // inner
    in_fwd = [(j, (j // inner) * inner + (j % inner + 1) % inner) for j in range(total)]
    in_bwd = [(j, (j // inner) * inner + (j % inner - 1) % inner) for j in range(total)]
    out_fwd = [(j, ((j // inner + 1) % outer) * inner + j % inner) for j in range(total)]
    out_bwd = [(j, ((j // inner - 1) % outer) * inner + j % inner) for j in range(total)]
    half = rows.shape[0] // 2
    first, second = rows[:half], rows[half:]
    first = sub_ring_gather(first, axis, inner, me_in, in_fwd, in_bwd)
    first = sub_ring_gather(first, axis, outer, me_out, out_fwd, out_bwd)
    second = sub_ring_gather(second, axis, outer, me_out, out_fwd, out_bwd)
    second = sub_ring_gather(second, axis, inner, me_in, in_fwd, in_bwd)
    second = jnp.swapaxes(second, 0, 1)
    both = jnp.concatenate([first, second], axis=2)
    return both.reshape((total * rows.shape[0],) + rows.shape[1:])


def a2a_gather(shard, axis, n):
    copies = jnp.broadcast_to(shard[None], (n,) + shard.shape)
    return lax.all_to_all(copies, axis, 0, 0, tiled=False)


def body(
    patches,
    image_number,
    patch_grid,
    first_gain,
    first_bias,
    attend_weight,
    output_weight,
    layer_scale,
    second_gain,
    second_bias,
    merge_weight,
    text_rows,
    prompt_source,
    final_gain,
    decoder_weight,
):
    fsdp_n = 8
    seq_n = 16
    patch_count = patches.shape[0]
    model_width = patches.shape[1]

    attend_flat = attend_weight.reshape(attend_weight.shape[0], -1)
    attend_cols = attend_flat.shape[1]
    shard_rows = attend_flat.shape[0]
    output_end = attend_cols + output_weight.shape[0]
    early = jnp.concatenate([attend_flat, output_weight.T, decoder_weight], axis=1)
    early_full, decoder_full = ring_gather(
        early, "fsdp", fsdp_n, [0, output_end, early.shape[1]]
    )
    attend_full = early_full[:, :, :attend_cols].reshape(-1, attend_cols)
    output_full = early_full[:, :, attend_cols:].reshape(-1, output_weight.shape[0]).T
    text_normed = rms_norm(text_rows, final_gain)

    inputs = patches.astype(jnp.float32)
    own_normed = layer_norm(inputs, first_gain, first_bias).astype(jnp.bfloat16)
    normed = lax.all_gather(own_normed, "seq", axis=0, tiled=True)
    after_normed = own_normed[0, 0] * 0
    text_all = lax.all_gather(text_normed + after_normed, "seq", axis=0, tiled=True)
    group_size = seq_n * patch_count
    head_block = attend_weight.shape[1]
    packed_width = attend_weight.shape[2]
    head_size = packed_width // 3
    packed = jnp.dot(normed, attend_full, preferred_element_type=jnp.float32)
    decoder_full = decoder_full + (packed[0, 0] * 0).astype(decoder_full.dtype)
    decoder_full = decoder_full.reshape(-1, decoder_weight.shape[1])
    packed = packed.astype(jnp.bfloat16).reshape(group_size, head_block, packed_width)
    queries = rotate(
        packed[..., :head_size].astype(jnp.float32), patch_grid[0], patch_grid[1]
    ).astype(jnp.bfloat16)
    keys_turned = rotate(
        packed[..., head_size : 2 * head_size].astype(jnp.float32), patch_grid[0], patch_grid[1]
    ).astype(jnp.bfloat16)
    values = packed[..., 2 * head_size :]
    scores = (
        jnp.einsum("qhd,khd->hqk", queries, keys_turned, preferred_element_type=jnp.float32)
        / float(head_size) ** 0.5
    )
    same_image = image_number[:, None] == image_number[None, :]
    scores = jnp.where(same_image[None], scores, -1e30)
    peaks = jnp.max(scores, axis=-1, keepdims=True)
    expos = jnp.exp(scores - peaks)
    weights = (expos / jnp.sum(expos, axis=-1, keepdims=True)).astype(jnp.bfloat16)
    mixed = jnp.einsum("hqk,khd->qhd", weights, values, preferred_element_type=jnp.float32)
    mixed = mixed.astype(jnp.bfloat16).reshape(group_size, head_block * head_size)
    partial_value = jnp.dot(mixed, output_full, preferred_element_type=jnp.float32)
    merge_cols = merge_weight.size // shard_rows
    late = merge_weight.reshape(shard_rows, merge_cols)
    partial_sent = partial_value.astype(jnp.bfloat16)
    corner = partial_sent[:1, :1] + text_all[:1, :1] * 0
    partial_sent = lax.dynamic_update_slice(partial_sent, corner, (0, 0))
    late = late + partial_sent[0, 0] * 0
    (late_full,) = ring_gather(late, "fsdp", fsdp_n)
    merge_full = late_full.reshape(-1, merge_weight.shape[1])

    text_projected = jnp.dot(text_all, decoder_full, preferred_element_type=jnp.float32)
    text_projected = text_projected.astype(jnp.bfloat16)
    summed = lax.psum_scatter(
        partial_sent, "seq", scatter_dimension=0, tiled=True
    ).astype(jnp.float32)
    vision_rows = (inputs + layer_scale * summed).astype(jnp.bfloat16)
    after_late = ((late_full[0, 0, 0] + late_full[0, -1, 0]) * 0).astype(jnp.float32)
    own_merged = layer_norm(vision_rows.astype(jnp.float32), second_gain + after_late, second_bias).astype(
        jnp.bfloat16
    )
    own_merged = own_merged.reshape(patch_count // 4, 4 * model_width)
    merged = lax.all_gather(own_merged, "seq", axis=0, tiled=True)
    image_cols = jnp.dot(merged, merge_full, preferred_element_type=jnp.float32)
    image_cols = image_cols.astype(jnp.bfloat16)
    token_count = image_cols.shape[0]
    block_width = image_cols.shape[1]
    image_blocks = a2a_gather(image_cols, "seq", seq_n)
    image_real = image_blocks.astype(jnp.float32)
    image_meansq = jnp.mean(image_real * image_real, axis=(0, 2), keepdims=True)
    image_normed = (
        image_real
        * lax.rsqrt(image_meansq + 1e-05)
        * final_gain.reshape(seq_n, 1, block_width)
    ).astype(jnp.bfloat16)
    image_projected = jnp.einsum(
        "stc,scn->tn",
        image_normed,
        decoder_full.reshape(seq_n, block_width, -1),
        preferred_element_type=jnp.float32,
    ).astype(jnp.bfloat16)
    is_image = prompt_source[:, None] >= 0
    pick = (prompt_source[:, None] == jnp.arange(token_count)[None, :]).astype(jnp.bfloat16)
    image_rows = jnp.dot(pick, image_projected, preferred_element_type=jnp.float32)
    projected = jnp.where(is_image, image_rows.astype(jnp.bfloat16), text_projected)
    return (vision_rows, projected)


def solution(mesh):
    return jax.shard_map(
        body,
        mesh=mesh,
        in_specs=(
            P(("fsdp", "seq"), None),
            P("fsdp"),
            P(None, "fsdp"),
            P(),
            P(),
            P("fsdp", "seq", None),
            P("seq", "fsdp"),
            P(),
            P(),
            P(),
            P("fsdp", "seq"),
            P(("fsdp", "seq"), None),
            P("fsdp"),
            P(),
            P("fsdp", "seq"),
        ),
        out_specs=(P(("fsdp", "seq"), None), P("fsdp", "seq")),
        check_vma=False,
    )
```

```python
import jax
import jax.numpy as jnp
from jax import lax
from jax.sharding import PartitionSpec as P


def layer_norm(values, factor, shifts):
    center = values - jnp.mean(values, axis=-1, keepdims=True)
    spread = jnp.mean(center * center, axis=-1, keepdims=True)
    return center * lax.rsqrt(spread + 1e-06) * factor + shifts


def rms_norm(rows, gain):
    realvals = rows.astype(jnp.float32)
    meansq = jnp.mean(realvals * realvals, axis=-1, keepdims=True)
    return (realvals * lax.rsqrt(meansq + 1e-05) * gain).astype(jnp.bfloat16)


def rotate(values, grid_rows, grid_cols):
    quarter = values.shape[-1] // 4
    frequency = 100.0 ** (-jnp.arange(quarter, dtype=jnp.float32) / quarter)
    pieces = []
    for offset, position in ((0, grid_rows), (2 * quarter, grid_cols)):
        angles = position.astype(jnp.float32)[:, None, None] * frequency
        cosine = jnp.cos(angles)
        sine_part = jnp.sin(angles)
        leading = values[..., offset : offset + quarter]
        trailing = values[..., offset + quarter : offset + 2 * quarter]
        pieces.append(leading * cosine - trailing * sine_part)
        pieces.append(leading * sine_part + trailing * cosine)
    return jnp.concatenate(pieces, axis=-1)


def ring_gather(shard, axis, n, bounds=None):
    me = lax.axis_index(axis)
    forward = [(j, (j + 1) % n) for j in range(n)]
    backward = [(j, (j - 1) % n) for j in range(n)]
    half = shard.shape[0] // 2
    ahead, behind = shard[:half], shard[half:]
    got_ahead = [ahead]
    got_behind = [behind]
    for _ in range(1, n):
        ahead = lax.ppermute(ahead, axis, forward)
        behind = lax.ppermute(behind, axis, backward)
        got_ahead.append(ahead)
        got_behind.append(behind)
    if bounds is None:
        bounds = [0, shard.shape[-1]]
    results = []
    for lo, hi in zip(bounds[:-1], bounds[1:]):
        from_ahead = jnp.stack([got_ahead[(-m) % n][..., lo:hi] for m in range(n)])
        from_behind = jnp.stack([got_behind[m][..., lo:hi] for m in range(n)])
        from_ahead = jnp.roll(from_ahead, me, axis=0)
        from_behind = jnp.roll(from_behind, me, axis=0)
        results.append(jnp.concatenate([from_ahead, from_behind], axis=1))
    return results


def sub_ring_gather(shard, axis, n, me, forward, backward):
    half = shard.shape[0] // 2
    ahead, behind = shard[:half], shard[half:]
    got_ahead = [ahead]
    got_behind = [behind]
    for _ in range(1, n):
        ahead = lax.ppermute(ahead, axis, forward)
        behind = lax.ppermute(behind, axis, backward)
        got_ahead.append(ahead)
        got_behind.append(behind)
    from_ahead = jnp.stack([got_ahead[(-m) % n] for m in range(n)])
    from_behind = jnp.stack(got_behind)
    from_ahead = jnp.roll(from_ahead, me, axis=0)
    from_behind = jnp.roll(from_behind, me, axis=0)
    return jnp.concatenate([from_ahead, from_behind], axis=1)


def torus_gather(rows, axis, inner):
    total = lax.axis_size(axis)
    outer = total // inner
    me = lax.axis_index(axis)
    me_in, me_out = me % inner, me // inner
    in_fwd = [(j, (j // inner) * inner + (j % inner + 1) % inner) for j in range(total)]
    in_bwd = [(j, (j // inner) * inner + (j % inner - 1) % inner) for j in range(total)]
    out_fwd = [(j, ((j // inner + 1) % outer) * inner + j % inner) for j in range(total)]
    out_bwd = [(j, ((j // inner - 1) % outer) * inner + j % inner) for j in range(total)]
    half = rows.shape[0] // 2
    first, second = rows[:half], rows[half:]
    first = sub_ring_gather(first, axis, inner, me_in, in_fwd, in_bwd)
    first = sub_ring_gather(first, axis, outer, me_out, out_fwd, out_bwd)
    second = sub_ring_gather(second, axis, outer, me_out, out_fwd, out_bwd)
    second = sub_ring_gather(second, axis, inner, me_in, in_fwd, in_bwd)
    second = jnp.swapaxes(second, 0, 1)
    both = jnp.concatenate([first, second], axis=2)
    return both.reshape((total * rows.shape[0],) + rows.shape[1:])


def a2a_gather(shard, axis, n):
    copies = jnp.broadcast_to(shard[None], (n,) + shard.shape)
    return lax.all_to_all(copies, axis, 0, 0, tiled=False)


def body(
    patches,
    image_number,
    patch_grid,
    first_gain,
    first_bias,
    attend_weight,
    output_weight,
    layer_scale,
    second_gain,
    second_bias,
    merge_weight,
    text_rows,
    prompt_source,
    final_gain,
    decoder_weight,
):
    fsdp_n = 8
    seq_n = 16
    patch_count = patches.shape[0]
    model_width = patches.shape[1]

    attend_flat = attend_weight.reshape(attend_weight.shape[0], -1)
    attend_cols = attend_flat.shape[1]
    shard_rows = attend_flat.shape[0]
    output_end = attend_cols + output_weight.shape[0]
    early = jnp.concatenate([attend_flat, output_weight.T, decoder_weight], axis=1)
    early_full, decoder_full = ring_gather(
        early, "fsdp", fsdp_n, [0, output_end, early.shape[1]]
    )
    attend_full = early_full[:, :, :attend_cols].reshape(-1, attend_cols)
    output_full = early_full[:, :, attend_cols:].reshape(-1, output_weight.shape[0]).T
    text_normed = rms_norm(text_rows, final_gain)

    inputs = patches.astype(jnp.float32)
    own_normed = layer_norm(inputs, first_gain, first_bias).astype(jnp.bfloat16)
    normed = lax.all_gather(own_normed, "seq", axis=0, tiled=True)
    after_normed = own_normed[0, 0] * 0
    text_all = lax.all_gather(text_normed + after_normed, "seq", axis=0, tiled=True)
    group_size = seq_n * patch_count
    head_block = attend_weight.shape[1]
    packed_width = attend_weight.shape[2]
    head_size = packed_width // 3
    packed = jnp.dot(normed, attend_full, preferred_element_type=jnp.float32)
    decoder_full = decoder_full + (packed[0, 0] * 0).astype(decoder_full.dtype)
    decoder_full = decoder_full.reshape(-1, decoder_weight.shape[1])
    packed = packed.astype(jnp.bfloat16).reshape(group_size, head_block, packed_width)
    queries = rotate(
        packed[..., :head_size].astype(jnp.float32), patch_grid[0], patch_grid[1]
    ).astype(jnp.bfloat16)
    keys_turned = rotate(
        packed[..., head_size : 2 * head_size].astype(jnp.float32), patch_grid[0], patch_grid[1]
    ).astype(jnp.bfloat16)
    values = packed[..., 2 * head_size :]
    scores = (
        jnp.einsum("qhd,khd->hqk", queries, keys_turned, preferred_element_type=jnp.float32)
        / float(head_size) ** 0.5
    )
    same_image = image_number[:, None] == image_number[None, :]
    scores = jnp.where(same_image[None], scores, -1e30)
    peaks = jnp.max(scores, axis=-1, keepdims=True)
    expos = jnp.exp(scores - peaks)
    weights = (expos / jnp.sum(expos, axis=-1, keepdims=True)).astype(jnp.bfloat16)
    mixed = jnp.einsum("hqk,khd->qhd", weights, values, preferred_element_type=jnp.float32)
    mixed = mixed.astype(jnp.bfloat16).reshape(group_size, head_block * head_size)
    partial_value = jnp.dot(mixed, output_full, preferred_element_type=jnp.float32)
    merge_cols = merge_weight.size // shard_rows
    late = merge_weight.reshape(shard_rows, merge_cols)
    partial_sent = partial_value.astype(jnp.bfloat16)
    corner = partial_sent[:1, :1] + text_all[:1, :1] * 0
    partial_sent = lax.dynamic_update_slice(partial_sent, corner, (0, 0))
    late = late + partial_sent[0, 0] * 0
    (late_full,) = ring_gather(late, "fsdp", fsdp_n)
    merge_full = late_full.reshape(-1, merge_weight.shape[1])

    text_projected = jnp.dot(text_all, decoder_full, preferred_element_type=jnp.float32)
    text_projected = text_projected.astype(jnp.bfloat16)
    summed = lax.psum_scatter(
        partial_sent, "seq", scatter_dimension=0, tiled=True
    ).astype(jnp.float32)
    vision_rows = (inputs + layer_scale * summed).astype(jnp.bfloat16)
    after_late = ((late_full[0, 0, 0] + late_full[0, -1, 0]) * 0).astype(jnp.float32)
    own_merged = layer_norm(vision_rows.astype(jnp.float32), second_gain + after_late, second_bias).astype(
        jnp.bfloat16
    )
    own_merged = own_merged.reshape(patch_count // 4, 4 * model_width)
    merged_rows = own_merged.shape[0]
    split = merged_rows // 2
    merged_first = lax.all_gather(own_merged[:split], "seq", axis=0, tiled=False)
    merged_second = a2a_gather(own_merged[split:], "seq", seq_n)
    image_first = jnp.einsum(
        "srk,kc->src", merged_first, merge_full, preferred_element_type=jnp.float32
    ).astype(jnp.bfloat16)
    image_second = jnp.einsum(
        "srk,kc->src", merged_second, merge_full, preferred_element_type=jnp.float32
    ).astype(jnp.bfloat16)
    image_cols = jnp.concatenate([image_first, image_second], axis=1)
    image_cols = image_cols.reshape(seq_n * merged_rows, -1)
    token_count = image_cols.shape[0]
    block_width = image_cols.shape[1]
    image_blocks = a2a_gather(image_cols, "seq", seq_n)
    image_real = image_blocks.astype(jnp.float32)
    image_meansq = jnp.mean(image_real * image_real, axis=(0, 2), keepdims=True)
    image_normed = (
        image_real
        * lax.rsqrt(image_meansq + 1e-05)
        * final_gain.reshape(seq_n, 1, block_width)
    ).astype(jnp.bfloat16)
    image_projected = jnp.einsum(
        "stc,scn->tn",
        image_normed,
        decoder_full.reshape(seq_n, block_width, -1),
        preferred_element_type=jnp.float32,
    ).astype(jnp.bfloat16)
    is_image = prompt_source[:, None] >= 0
    pick = (prompt_source[:, None] == jnp.arange(token_count)[None, :]).astype(jnp.bfloat16)
    image_rows = jnp.dot(pick, image_projected, preferred_element_type=jnp.float32)
    projected = jnp.where(is_image, image_rows.astype(jnp.bfloat16), text_projected)
    return (vision_rows, projected)


def solution(mesh):
    return jax.shard_map(
        body,
        mesh=mesh,
        in_specs=(
            P(("fsdp", "seq"), None),
            P("fsdp"),
            P(None, "fsdp"),
            P(),
            P(),
            P("fsdp", "seq", None),
            P("seq", "fsdp"),
            P(),
            P(),
            P(),
            P("fsdp", "seq"),
            P(("fsdp", "seq"), None),
            P("fsdp"),
            P(),
            P("fsdp", "seq"),
        ),
        out_specs=(P(("fsdp", "seq"), None), P("fsdp", "seq")),
        check_vma=False,
    )
```
